256 devices in a mesh: req: 128 (over x, y, z), tp: 2 (over core).
Axes of the slice: x: 4, y: 4, z: 8, core: 2. Of those that a mesh axis runs over, the one named last changes fastest.
Arguments:
- tokens: bfloat16 [65536, 1024], P('req'), may hold values from -6 to 6
- group_len: int32 [128], P('req'), may hold values from 1 to 512, 49152 in all
- cache_len: int32 [128], replicated, may hold values from 1 to 1024, 65536 in all
- cache_keys: bfloat16 [128, 1024, 1024], P('req', None, 'tp'), may hold values from -192 to 192
- cache_values: bfloat16 [128, 1024, 1024], P('req', None, 'tp'), may hold values from -6 to 6
- w_query: bfloat16 [1024, 1024], P(None, 'tp'), may hold values from -0.1875 to 0.1875
- w_key: bfloat16 [1024, 1024], P(None, 'tp'), may hold values from -0.1875 to 0.1875
- w_value: bfloat16 [1024, 1024], P(None, 'tp'), may hold values from -0.1875 to 0.1875
- w_out: bfloat16 [1024, 1024], P('tp'), may hold values from -0.1875 to 0.1875
- w_up: bfloat16 [1024, 2048], P(None, 'tp'), may hold values from -0.1875 to 0.1875
- w_down: bfloat16 [2048, 1024], P('tp'), may hold values from -0.125 to 0.125
- ln_gains: float32 [2, 1024], replicated, may hold values from 0.5 to 1.5
- ln_biases: float32 [2, 1024], replicated, may hold values from -3 to 3
- embed: bfloat16 [49152, 1024], P(('req', 'tp')), may hold values from -0.5 to 0.5
Outputs:
- layer_out: bfloat16 [65536, 1024], P('req')
- top_logit: float32 [128], P('req')
- shard_top: float32 [128, 256], P(None, ('req', 'tp'))
The draws below stay inside these ranges and needn't reach their ends.
Inputs may be any that keep to these rules, and one draw needn't show every extreme that they name: `cache_len`: one request has exactly 1024 cached positions. `group_len`: one request has a full block of 512 valid tokens.
All inputs are finite; a program needn't handle non-finite values.
Results may differ from the reference program's by a relative error of at most 0.015.
Values may be sent and summed in bfloat16 or wider, within the bound.
No kernel may reach another device: no remote copies, remote signals or barrier semaphores. Data moves between devices by JAX's collectives and lax.ppermute only.
A program may use at most 128 MiB of HBM per device.

```python
import math
import jax
import jax.numpy as jnp
import numpy as np
from jax import lax

D = 1024
HEADS = 16
HD = 64
FF = 2048
VOCAB = 49152
CH = 512
CMAX = 1024
REQS = 128
TOKENS = 65536
SHARDS = 256


def draw_cache_keys(key, part):
    first_key = jax.random.fold_in(jax.random.fold_in(key, 11), 0)
    third_key = jax.random.fold_in(jax.random.fold_in(key, 11), 2)
    fourth_key = jax.random.fold_in(jax.random.fold_in(key, 11), 3)
    values = jnp.clip(jax.random.normal(first_key, (REQS, CMAX, D), jnp.float32), -6.0, 6.0)
    strength = 30.0 * jnp.exp(jax.random.uniform(fourth_key, (REQS, 1, 1), jnp.float32) * jnp.log(3.0))
    leading = jnp.clip(jax.random.normal(third_key, (REQS, 1, D), jnp.float32), -2.0, 2.0) * strength
    paired = jnp.concatenate([leading, leading * 1.02], axis=1)
    values = jnp.concatenate([paired, values[:, 2:]], axis=1)
    return values.astype(jnp.bfloat16)


def shard_levels(key, dims, shards, least, largest):
    loudness, own = 1.0, jax.random.fold_in(key, 6)
    for axis_at, parts in shards:
        steps = jnp.exp(jax.random.uniform(jax.random.fold_in(own, axis_at), (parts,), jnp.float32, least / len(shards), largest / len(shards)))
        loudness = loudness * jnp.repeat(steps, dims[axis_at] // parts).reshape([-1 if axis == axis_at else 1 for axis in range(len(dims))])
    return loudness


def length_profile(count, total, reach, slope):
    loads = [(1 << 20) // math.isqrt(standing ** slope) + 1 for standing in range(2, count + 1)]
    surplus, given = total - reach - (count - 1), [1] * (count - 1)
    while surplus > 0:
        free = [i for i in range(count - 1) if given[i] < reach]
        mass, remaining = sum([loads[i] for i in free]), surplus
        for i in free:
            extra = min(reach - given[i], max(1, remaining * loads[i] // mass), surplus)
            given[i] = given[i] + extra
            surplus = surplus - extra
    return np.array([reach] + given)


def uneven(stream_key, count, total, bound, lean):
    if count == 2:
        one = jax.random.randint(stream_key, (), max(1, total - bound), min(bound, total - 1) + 1)
        return jnp.stack([one, total - one])
    lengths = jnp.asarray(length_profile(count, total, bound, lean), jnp.int32)
    pairs = (count - 1) // 2
    giver, sink = lengths[1:1 + 2 * pairs:2], lengths[2:2 + 2 * pairs:2]
    slack = jnp.minimum(giver - 1, bound - sink)
    moved = jax.random.randint(jax.random.fold_in(stream_key, 1), (pairs,), 0, 1 << 20) % (slack + 1)
    lengths = lengths.at[1:1 + 2 * pairs:2].set(giver - moved).at[2:2 + 2 * pairs:2].set(sink + moved)
    return lengths[jax.random.permutation(jax.random.fold_in(stream_key, 2), count)]


def noise(stream_key, shape, deviation, limit, cuts=(), kind=jnp.bfloat16):
    drawn = deviation * jax.random.normal(stream_key, shape, jnp.float32)
    if cuts:
        drawn = drawn * shard_levels(stream_key, shape, cuts, -0.22, 0.18)
    return jnp.clip(drawn, -limit, limit).astype(kind)


def setup_inputs(seed: int = 0) -> dict:
    arg_keys = jax.random.split(jax.random.key(seed), 15)
    return {
        "tokens": noise(arg_keys[0], (TOKENS, D), 1.0, 6.0, ((0, 128),)),
        "group_len": uneven(arg_keys[1], REQS, REQS * CH * 3 // 4, CH, 1).astype(jnp.int32),
        "cache_len": uneven(arg_keys[2], REQS, REQS * CMAX // 2, CMAX, 2).astype(jnp.int32),
        "cache_keys": draw_cache_keys(jax.random.fold_in(arg_keys[14], 71), 0),
        "cache_values": noise(arg_keys[4], (REQS, CMAX, D), 1.0, 6.0, ((0, 128), (2, 2))),
        "w_query": noise(arg_keys[5], (D, D), D ** -0.5, 0.1875, ((1, 2),)),
        "w_key": noise(arg_keys[6], (D, D), D ** -0.5, 0.1875, ((1, 2),)),
        "w_value": noise(arg_keys[7], (D, D), D ** -0.5, 0.1875, ((1, 2),)),
        "w_out": noise(arg_keys[8], (D, D), D ** -0.5, 0.1875, ((0, 2),)),
        "w_up": noise(arg_keys[9], (D, FF), D ** -0.5, 0.1875, ((1, 2),)),
        "w_down": noise(arg_keys[10], (FF, D), FF ** -0.5, 0.125, ((0, 2),)),
        "ln_gains": jnp.clip(1.0 + 0.1 * jax.random.normal(arg_keys[11], (2, D), jnp.float32), 0.5, 1.5),
        "ln_biases": noise(arg_keys[12], (2, D), 0.5, 3.0, (), jnp.float32),
        "embed": noise(arg_keys[13], (VOCAB, D), (D // 9) ** -0.5, 0.5, ((0, 256),)),
    }


def normalize(rows, gain, bias):
    center = rows - lax.optimization_barrier(jnp.mean(rows, axis=-1, keepdims=True))
    spread = lax.optimization_barrier(jnp.mean(center * center, axis=-1, keepdims=True))
    return center * lax.rsqrt(spread + 1e-05) * gain + bias

def reference(tokens, group_len, cache_len, cache_keys, cache_values, w_query, w_key, w_value, w_out, w_up, w_down, ln_gains, ln_biases, embed):
    groups = tokens.reshape(REQS, CH, D)

    def per_request(items):
        group_rows, old_keys, old_values, cached, valid = items
        queries = jnp.dot(group_rows, w_query, preferred_element_type=jnp.float32).astype(jnp.bfloat16).reshape(CH, HEADS, HD)
        keys_new = jnp.dot(group_rows, w_key, preferred_element_type=jnp.float32).astype(jnp.bfloat16)
        values_new = jnp.dot(group_rows, w_value, preferred_element_type=jnp.float32).astype(jnp.bfloat16)
        all_keys = jnp.concatenate([old_keys, keys_new], axis=0).reshape(CMAX + CH, HEADS, HD)
        all_values = jnp.concatenate([old_values, values_new], axis=0).reshape(CMAX + CH, HEADS, HD)
        scores = jnp.einsum('qhd,khd->qhk', queries.astype(jnp.float32), all_keys.astype(jnp.float32)) / jnp.sqrt(jnp.float32(HD))
        places = jnp.arange(CMAX + CH, dtype=jnp.int32)
        row_ids = jnp.arange(CH, dtype=jnp.int32)
        in_block = places - CMAX
        allowed = jnp.where((places < CMAX)[None, :], (places < cached)[None, :], (in_block[None, :] <= row_ids[:, None]) & (in_block < valid)[None, :])
        scores = jnp.where(allowed[:, None, :], scores, -jnp.inf)
        row_peak = lax.optimization_barrier(jnp.max(scores, axis=-1, keepdims=True))
        raised = jnp.exp(scores - row_peak)
        row_total = lax.optimization_barrier(jnp.sum(raised, axis=-1))
        rounded = lax.optimization_barrier(raised.astype(jnp.bfloat16)).astype(jnp.float32)
        attended = jnp.einsum('qhk,khd->qhd', rounded, all_values.astype(jnp.float32)) / row_total[..., None]
        attended = attended.astype(jnp.bfloat16).reshape(CH, D)
        hidden = group_rows.astype(jnp.float32) + jnp.dot(attended, w_out, preferred_element_type=jnp.float32)
        middle = normalize(hidden, ln_gains[0], ln_biases[0]).astype(jnp.bfloat16)
        active = jax.nn.gelu(jnp.dot(middle, w_up, preferred_element_type=jnp.float32), approximate=False).astype(jnp.bfloat16)
        summed = middle.astype(jnp.float32) + jnp.dot(active, w_down, preferred_element_type=jnp.float32)
        layer_rows = normalize(summed, ln_gains[1], ln_biases[1]).astype(jnp.bfloat16)
        last_row = lax.dynamic_slice_in_dim(layer_rows, (valid - 1).astype(jnp.int32), 1, 0)[0]
        return (layer_rows, last_row)
    layer_rows, last_rows = lax.map(per_request, (groups, cache_keys, cache_values, cache_len, group_len))
    logits = jnp.dot(last_rows, embed.T, preferred_element_type=jnp.float32)
    shard_top = lax.optimization_barrier(jnp.max(logits.reshape(REQS, SHARDS, VOCAB // SHARDS), axis=2))
    return (layer_rows.reshape(REQS * CH, D), lax.optimization_barrier(jnp.max(shard_top, axis=1)), shard_top)
```

```python
import jax
import jax.numpy as jnp
from jax import lax
from jax.sharding import PartitionSpec as P

HD = 64
BLK = 256


start_peak = -1e30


def normalize(rows, gain, bias):
    center = rows - jnp.mean(rows, axis=-1, keepdims=True)
    spread = jnp.mean(center * center, axis=-1, keepdims=True)
    return center * lax.rsqrt(spread + 1e-05) * gain + bias


def pair_sum(partial):
    own = partial.astype(jnp.bfloat16)
    other = lax.ppermute(own, "tp", [(0, 1), (1, 0)])
    return own.astype(jnp.float32) + other.astype(jnp.float32)


def attend(soft_state, queries, keys_blk, values_blk, allowed):
    row_peak, row_total, accum = soft_state
    scale = 1.0 / jnp.sqrt(jnp.float32(queries.shape[2]))
    scores = (
        jnp.einsum("qhd,khd->qhk", queries, keys_blk, preferred_element_type=jnp.float32) * scale
    )
    scores = jnp.where(allowed[:, None, :], scores, -jnp.inf)
    new_peak = jnp.maximum(row_peak, jnp.max(scores, axis=-1))
    factor = jnp.exp(row_peak - new_peak)
    raised = jnp.exp(scores - new_peak[..., None])
    new_total = row_total * factor + jnp.sum(raised, axis=-1)
    new_accum = accum * factor[..., None] + jnp.einsum(
        "qhk,khd->qhd", raised.astype(jnp.bfloat16), values_blk, preferred_element_type=jnp.float32
    )
    return (new_peak, new_total, new_accum)


def cache_pass(soft_state, queries, keys_all, values_all, offset, blocks, length):

    def one_block(block_idx, carry):
        keys_blk = lax.dynamic_slice_in_dim(keys_all, block_idx * BLK, BLK, 0)
        values_blk = lax.dynamic_slice_in_dim(values_all, block_idx * BLK, BLK, 0)
        places = offset + block_idx * BLK + jnp.arange(BLK, dtype=jnp.int32)
        return attend(carry, queries, keys_blk, values_blk, (places < length)[None, :])

    return lax.fori_loop(jnp.int32(0), blocks, one_block, soft_state)


def shards(
    tokens,
    group_len,
    cache_len,
    cache_keys,
    cache_values,
    w_query,
    w_key,
    w_value,
    w_out,
    w_up,
    w_down,
    ln_gains,
    ln_biases,
    embed,
):
    block_rows = tokens.shape[0]
    local_width = w_query.shape[1]
    heads_local = local_width // HD
    cache_rows = cache_keys.shape[1]
    my_index = lax.axis_index("req")
    my_cache = lax.dynamic_index_in_dim(cache_len, my_index, 0, keepdims=False)
    my_valid = group_len[0]
    queries = jnp.dot(tokens, w_query, preferred_element_type=jnp.float32).astype(jnp.bfloat16)
    keys_new = jnp.dot(tokens, w_key, preferred_element_type=jnp.float32).astype(jnp.bfloat16)
    values_new = jnp.dot(tokens, w_value, preferred_element_type=jnp.float32).astype(jnp.bfloat16)
    head_queries = queries.reshape(block_rows, heads_local, HD)
    empty_state = (
        jnp.full((block_rows, heads_local), start_peak, jnp.float32),
        jnp.zeros((block_rows, heads_local), jnp.float32),
        jnp.zeros((block_rows, heads_local, HD), jnp.float32),
    )
    row_ids = jnp.arange(block_rows, dtype=jnp.int32)
    block_allowed = (row_ids[None, :] <= row_ids[:, None]) & (row_ids < my_valid)[None, :]
    soft_state = attend(
        empty_state,
        head_queries,
        keys_new.reshape(block_rows, heads_local, HD),
        values_new.reshape(block_rows, heads_local, HD),
        block_allowed,
    )
    own_keys = cache_keys[0].reshape(cache_rows, heads_local, HD)
    own_values = cache_values[0].reshape(cache_rows, heads_local, HD)
    own_blocks = (my_cache + BLK - 1) // BLK
    soft_state = cache_pass(soft_state, head_queries, own_keys, own_values, 0, own_blocks, my_cache)
    attn_mixed = (
        (soft_state[2] / soft_state[1][..., None])
        .astype(jnp.bfloat16)
        .reshape(block_rows, local_width)
    )
    attn_sum = pair_sum(jnp.dot(attn_mixed, w_out, preferred_element_type=jnp.float32))
    middle = normalize(tokens.astype(jnp.float32) + attn_sum, ln_gains[0], ln_biases[0]).astype(
        jnp.bfloat16
    )
    active = jax.nn.gelu(
        jnp.dot(middle, w_up, preferred_element_type=jnp.float32), approximate=False
    ).astype(jnp.bfloat16)
    ffn_sum = pair_sum(jnp.dot(active, w_down, preferred_element_type=jnp.float32))
    layer_out = normalize(middle.astype(jnp.float32) + ffn_sum, ln_gains[1], ln_biases[1]).astype(
        jnp.bfloat16
    )
    last_row = lax.dynamic_slice_in_dim(layer_out, my_valid - 1, 1, 0)
    reqs = cache_len.shape[0]
    all_rows = lax.all_to_all(
        jnp.broadcast_to(last_row, (reqs, last_row.shape[1])), "req", 0, 0, tiled=True
    )
    logits = jnp.einsum("rd,vd->rv", all_rows, embed, preferred_element_type=jnp.float32)
    slice_best = jnp.max(logits, axis=1)
    mine = jnp.max(lax.all_to_all(slice_best[:, None], "req", 0, 0, tiled=True), axis=0)
    best_logit = jnp.maximum(mine, lax.ppermute(mine, "tp", [(0, 1), (1, 0)]))
    return (layer_out, best_logit, slice_best[:, None])


def solution(mesh):
    placed = (
        P("req", None),
        P("req"),
        P(),
        P("req", None, "tp"),
        P("req", None, "tp"),
        P(None, "tp"),
        P(None, "tp"),
        P(None, "tp"),
        P("tp", None),
        P(None, "tp"),
        P("tp", None),
        P(),
        P(),
        P(("req", "tp"), None),
    )
    return jax.shard_map(
        shards,
        mesh=mesh,
        in_specs=placed,
        out_specs=(P("req", None), P("req"), P(None, ("req", "tp"))),
        check_vma=False,
    )
```

```python
import jax
import jax.numpy as jnp
from jax import lax
from jax.sharding import PartitionSpec as P

HD = 64
BLK = 256


start_peak = -1e30


def normalize(rows, gain, bias):
    center = rows - jnp.mean(rows, axis=-1, keepdims=True)
    spread = jnp.mean(center * center, axis=-1, keepdims=True)
    return center * lax.rsqrt(spread + 1e-05) * gain + bias


def pair_sum(partial):
    own = partial.astype(jnp.bfloat16)
    other = lax.ppermute(own, "tp", [(0, 1), (1, 0)])
    return own.astype(jnp.float32) + other.astype(jnp.float32)


def attend(soft_state, queries, keys_blk, values_blk, allowed):
    row_peak, row_total, accum = soft_state
    scale = 1.0 / jnp.sqrt(jnp.float32(queries.shape[2]))
    scores = (
        jnp.einsum("qhd,khd->qhk", queries, keys_blk, preferred_element_type=jnp.float32) * scale
    )
    scores = jnp.where(allowed[:, None, :], scores, -jnp.inf)
    new_peak = jnp.maximum(row_peak, jnp.max(scores, axis=-1))
    factor = jnp.exp(row_peak - new_peak)
    raised = jnp.exp(scores - new_peak[..., None])
    new_total = row_total * factor + jnp.sum(raised, axis=-1)
    new_accum = accum * factor[..., None] + jnp.einsum(
        "qhk,khd->qhd", raised.astype(jnp.bfloat16), values_blk, preferred_element_type=jnp.float32
    )
    return (new_peak, new_total, new_accum)


def cache_pass(soft_state, queries, keys_all, values_all, offset, blocks, length):

    def one_block(block_idx, carry):
        keys_blk = lax.dynamic_slice_in_dim(keys_all, block_idx * BLK, BLK, 0)
        values_blk = lax.dynamic_slice_in_dim(values_all, block_idx * BLK, BLK, 0)
        places = offset + block_idx * BLK + jnp.arange(BLK, dtype=jnp.int32)
        return attend(carry, queries, keys_blk, values_blk, (places < length)[None, :])

    return lax.fori_loop(jnp.int32(0), blocks, one_block, soft_state)


def shards(
    tokens,
    group_len,
    cache_len,
    cache_keys,
    cache_values,
    w_query,
    w_key,
    w_value,
    w_out,
    w_up,
    w_down,
    ln_gains,
    ln_biases,
    embed,
):
    block_rows = tokens.shape[0]
    local_width = w_query.shape[1]
    heads_local = local_width // HD
    cache_rows = cache_keys.shape[1]
    my_index = lax.axis_index("req")
    my_cache = lax.dynamic_index_in_dim(cache_len, my_index, 0, keepdims=False)
    my_valid = group_len[0]
    queries = jnp.dot(tokens, w_query, preferred_element_type=jnp.float32).astype(jnp.bfloat16)
    keys_new = jnp.dot(tokens, w_key, preferred_element_type=jnp.float32).astype(jnp.bfloat16)
    values_new = jnp.dot(tokens, w_value, preferred_element_type=jnp.float32).astype(jnp.bfloat16)
    head_queries = queries.reshape(block_rows, heads_local, HD)
    empty_state = (
        jnp.full((block_rows, heads_local), start_peak, jnp.float32),
        jnp.zeros((block_rows, heads_local), jnp.float32),
        jnp.zeros((block_rows, heads_local, HD), jnp.float32),
    )
    row_ids = jnp.arange(block_rows, dtype=jnp.int32)
    block_allowed = (row_ids[None, :] <= row_ids[:, None]) & (row_ids < my_valid)[None, :]
    soft_state = attend(
        empty_state,
        head_queries,
        keys_new.reshape(block_rows, heads_local, HD),
        values_new.reshape(block_rows, heads_local, HD),
        block_allowed,
    )
    own_keys = cache_keys[0].reshape(cache_rows, heads_local, HD)
    own_values = cache_values[0].reshape(cache_rows, heads_local, HD)
    own_blocks = (my_cache + BLK - 1) // BLK
    soft_state = cache_pass(soft_state, head_queries, own_keys, own_values, 0, own_blocks, my_cache)
    attn_mixed = (
        (soft_state[2] / soft_state[1][..., None])
        .astype(jnp.bfloat16)
        .reshape(block_rows, local_width)
    )
    layer_out = finish_rows(attn_mixed, tokens, w_out, w_up, w_down, ln_gains, ln_biases)

    reqs = cache_len.shape[0]
    last = my_valid - 1
    q_last = lax.dynamic_slice_in_dim(head_queries, last, 1, 0)[0].astype(jnp.float32)
    keys_all = jnp.concatenate([own_keys, keys_new.reshape(block_rows, heads_local, HD)], axis=0)
    values_all = jnp.concatenate([own_values, values_new.reshape(block_rows, heads_local, HD)], axis=0)
    scale = 1.0 / jnp.sqrt(jnp.float32(HD))
    scores = jnp.einsum("hd,khd->hk", q_last, keys_all.astype(jnp.float32)) * scale
    places = jnp.arange(cache_rows + block_rows, dtype=jnp.int32)
    allowed = jnp.where(places < cache_rows, places < my_cache, places - cache_rows < my_valid)
    scores = jnp.where(allowed[None, :], scores, -jnp.inf)
    peak = jnp.max(scores, axis=-1, keepdims=True)
    raised = jnp.exp(scores - peak)
    total = jnp.sum(raised, axis=-1, keepdims=True)
    rounded = raised.astype(jnp.bfloat16).astype(jnp.float32)
    row_mixed = (jnp.einsum("hk,khd->hd", rounded, values_all.astype(jnp.float32)) / total).astype(
        jnp.bfloat16
    ).reshape(1, local_width)
    token_row = lax.dynamic_slice_in_dim(tokens, last, 1, 0)
    last_row = finish_rows(row_mixed, token_row, w_out, w_up, w_down, ln_gains, ln_biases)

    all_rows = gather_rows(last_row, reqs)
    logits = jnp.einsum("rd,vd->rv", all_rows, embed, preferred_element_type=jnp.float32)
    slice_best = jnp.max(logits, axis=1)
    best_all = max_everywhere(slice_best, reqs)
    best_logit = lax.dynamic_slice_in_dim(best_all, my_index, 1, 0)
    return (layer_out, best_logit, slice_best[:, None])


def finish_rows(attn_mixed, tokens, w_out, w_up, w_down, ln_gains, ln_biases):
    attn_sum = pair_sum(jnp.dot(attn_mixed, w_out, preferred_element_type=jnp.float32))
    middle = normalize(tokens.astype(jnp.float32) + attn_sum, ln_gains[0], ln_biases[0]).astype(
        jnp.bfloat16
    )
    active = jax.nn.gelu(
        jnp.dot(middle, w_up, preferred_element_type=jnp.float32), approximate=False
    ).astype(jnp.bfloat16)
    ffn_sum = pair_sum(jnp.dot(active, w_down, preferred_element_type=jnp.float32))
    return normalize(middle.astype(jnp.float32) + ffn_sum, ln_gains[1], ln_biases[1]).astype(
        jnp.bfloat16
    )


def gather_rows(row, count):
    me = lax.axis_index("req")
    held = row
    step = 1
    while step < count:
        other = lax.ppermute(held, "req", [(i, i ^ step) for i in range(count)])
        low = (me // step) % 2 == 0
        held = jnp.where(
            low, jnp.concatenate([held, other], axis=0), jnp.concatenate([other, held], axis=0)
        )
        step *= 2
    return held


def max_everywhere(values, count):
    values = jnp.maximum(values, lax.ppermute(values, "tp", [(0, 1), (1, 0)]))
    step = 1
    while step < count:
        values = jnp.maximum(values, lax.ppermute(values, "req", [(i, i ^ step) for i in range(count)]))
        step *= 2
    return values


def solution(mesh):
    placed = (
        P("req", None),
        P("req"),
        P(),
        P("req", None, "tp"),
        P("req", None, "tp"),
        P(None, "tp"),
        P(None, "tp"),
        P(None, "tp"),
        P("tp", None),
        P(None, "tp"),
        P("tp", None),
        P(),
        P(),
        P(("req", "tp"), None),
    )
    return jax.shard_map(
        shards,
        mesh=mesh,
        in_specs=placed,
        out_specs=(P("req", None), P("req"), P(None, ("req", "tp"))),
        check_vma=False,
    )
```

```python
import jax
import jax.numpy as jnp
from jax import lax
from jax.experimental import pallas as pl
from jax.experimental.pallas import tpu as pltpu
from jax.sharding import PartitionSpec as P

HD = 64


def normalize(rows, gain, bias):
    center = rows - jnp.mean(rows, axis=-1, keepdims=True)
    spread = jnp.mean(center * center, axis=-1, keepdims=True)
    return center * lax.rsqrt(spread + 1e-05) * gain + bias


def pair_sum(partial):
    own = partial.astype(jnp.bfloat16)
    other = lax.ppermute(own, "tp", [(0, 1), (1, 0)])
    return own.astype(jnp.float32) + other.astype(jnp.float32)


PAIR = 2 * HD
ROWS = 256


def attention_kernel(lens_ref, q_ref, kc_ref, vc_ref, kn_ref, vn_ref, out_ref):
    cached = lens_ref[0]
    valid = lens_ref[1]
    row0 = pl.program_id(1) * ROWS
    q = q_ref[...]
    kc = kc_ref[...]
    vc = vc_ref[...]
    kn = kn_ref[...]
    vn = vn_ref[...]
    lanes = lax.broadcasted_iota(jnp.int32, q.shape, 1)
    cache_cols = lax.broadcasted_iota(jnp.int32, (q.shape[0], kc.shape[0]), 1)
    cache_ok = cache_cols < cached
    new_cols = lax.broadcasted_iota(jnp.int32, (q.shape[0], kn.shape[0]), 1)
    new_rows = lax.broadcasted_iota(jnp.int32, (q.shape[0], kn.shape[0]), 0) + row0
    new_ok = (new_cols <= new_rows) & (new_cols < valid)
    scale = 1.0 / float(HD) ** 0.5
    dims = (((1,), (1,)), ((), ()))
    result = jnp.zeros(q.shape, jnp.float32)
    for head in range(2):
        mine = (lanes // HD) == head
        qh = jnp.where(mine, q, jnp.zeros_like(q))
        s_c = lax.dot_general(qh, kc, dims, preferred_element_type=jnp.float32) * scale
        s_n = lax.dot_general(qh, kn, dims, preferred_element_type=jnp.float32) * scale
        s_c = jnp.where(cache_ok, s_c, -jnp.inf)
        s_n = jnp.where(new_ok, s_n, -jnp.inf)
        peak = jnp.maximum(jnp.max(s_c, axis=1, keepdims=True), jnp.max(s_n, axis=1, keepdims=True))
        e_c = jnp.exp(s_c - peak)
        e_n = jnp.exp(s_n - peak)
        total = jnp.sum(e_c, axis=1, keepdims=True) + jnp.sum(e_n, axis=1, keepdims=True)
        mixed = jnp.dot(e_c.astype(jnp.bfloat16), vc, preferred_element_type=jnp.float32) + jnp.dot(
            e_n.astype(jnp.bfloat16), vn, preferred_element_type=jnp.float32
        )
        result = jnp.where(mine, mixed / total, result)
    out_ref[...] = result.astype(out_ref.dtype)


def attention(lens, queries, cache_k, cache_v, keys_new, values_new):
    rows, width = queries.shape
    cache_rows = cache_k.shape[0]
    pairs = width // PAIR
    chunks = rows // ROWS
    flops = 4 * rows * (cache_rows + rows) * width * 2
    return pl.pallas_call(
        attention_kernel,
        out_shape=jax.ShapeDtypeStruct((rows, width), jnp.bfloat16),
        grid_spec=pltpu.PrefetchScalarGridSpec(
            num_scalar_prefetch=1,
            grid=(pairs, chunks),
            in_specs=[
                pl.BlockSpec((ROWS, PAIR), lambda p, r, lens: (r, p)),
                pl.BlockSpec((cache_rows, PAIR), lambda p, r, lens: (0, p)),
                pl.BlockSpec((cache_rows, PAIR), lambda p, r, lens: (0, p)),
                pl.BlockSpec((rows, PAIR), lambda p, r, lens: (0, p)),
                pl.BlockSpec((rows, PAIR), lambda p, r, lens: (0, p)),
            ],
            out_specs=pl.BlockSpec((ROWS, PAIR), lambda p, r, lens: (r, p)),
        ),
        cost_estimate=pl.CostEstimate(
            flops=flops,
            transcendentals=rows * (cache_rows + rows) * width // HD,
            bytes_accessed=2 * (2 * rows * width + 2 * cache_rows * width + 2 * rows * width),
        ),
    )(lens, queries, cache_k, cache_v, keys_new, values_new)


def shards(
    tokens,
    group_len,
    cache_len,
    cache_keys,
    cache_values,
    w_query,
    w_key,
    w_value,
    w_out,
    w_up,
    w_down,
    ln_gains,
    ln_biases,
    embed,
):
    block_rows = tokens.shape[0]
    local_width = w_query.shape[1]
    my_index = lax.axis_index("req")
    my_cache = lax.dynamic_index_in_dim(cache_len, my_index, 0, keepdims=False)
    my_valid = group_len[0]
    queries = jnp.dot(tokens, w_query, preferred_element_type=jnp.float32).astype(jnp.bfloat16)
    keys_new = jnp.dot(tokens, w_key, preferred_element_type=jnp.float32).astype(jnp.bfloat16)
    values_new = jnp.dot(tokens, w_value, preferred_element_type=jnp.float32).astype(jnp.bfloat16)
    lens = jnp.stack([my_cache, my_valid]).astype(jnp.int32)
    attn_mixed = attention(lens, queries, cache_keys[0], cache_values[0], keys_new, values_new)
    attn_sum = pair_sum(jnp.dot(attn_mixed, w_out, preferred_element_type=jnp.float32))
    middle = normalize(tokens.astype(jnp.float32) + attn_sum, ln_gains[0], ln_biases[0]).astype(
        jnp.bfloat16
    )
    active = jax.nn.gelu(
        jnp.dot(middle, w_up, preferred_element_type=jnp.float32), approximate=False
    ).astype(jnp.bfloat16)
    ffn_sum = pair_sum(jnp.dot(active, w_down, preferred_element_type=jnp.float32))
    layer_out = normalize(middle.astype(jnp.float32) + ffn_sum, ln_gains[1], ln_biases[1]).astype(
        jnp.bfloat16
    )
    last_row = lax.dynamic_slice_in_dim(layer_out, my_valid - 1, 1, 0)
    reqs = cache_len.shape[0]
    all_rows = lax.all_to_all(
        jnp.broadcast_to(last_row, (reqs, last_row.shape[1])), "req", 0, 0, tiled=True
    )
    logits = jnp.einsum("rd,vd->rv", all_rows, embed, preferred_element_type=jnp.float32)
    slice_best = jnp.max(logits, axis=1)
    mine = jnp.max(lax.all_to_all(slice_best[:, None], "req", 0, 0, tiled=True), axis=0)
    best_logit = jnp.maximum(mine, lax.ppermute(mine, "tp", [(0, 1), (1, 0)]))
    return (layer_out, best_logit, slice_best[:, None])


def solution(mesh):
    placed = (
        P("req", None),
        P("req"),
        P(),
        P("req", None, "tp"),
        P("req", None, "tp"),
        P(None, "tp"),
        P(None, "tp"),
        P(None, "tp"),
        P("tp", None),
        P(None, "tp"),
        P("tp", None),
        P(),
        P(),
        P(("req", "tp"), None),
    )
    return jax.shard_map(
        shards,
        mesh=mesh,
        in_specs=placed,
        out_specs=(P("req", None), P("req"), P(None, ("req", "tp"))),
        check_vma=False,
    )
```

```python
import jax
import jax.numpy as jnp
from jax import lax
from jax.experimental import pallas as pl
from jax.experimental.pallas import tpu as pltpu
from jax.sharding import PartitionSpec as P

HD = 64


def normalize(rows, gain, bias):
    center = rows - jnp.mean(rows, axis=-1, keepdims=True)
    spread = jnp.mean(center * center, axis=-1, keepdims=True)
    return center * lax.rsqrt(spread + 1e-05) * gain + bias


def pair_sum(partial):
    own = partial.astype(jnp.bfloat16)
    other = lax.ppermute(own, "tp", [(0, 1), (1, 0)])
    return own.astype(jnp.float32) + other.astype(jnp.float32)


PAIR = 2 * HD
ROWS = 256


def attention_kernel(lens_ref, q_ref, kc_ref, vc_ref, kn_ref, vn_ref, out_ref):
    cached = lens_ref[0]
    valid = lens_ref[1]
    row0 = pl.program_id(1) * ROWS
    q = q_ref[...]
    kc = kc_ref[...]
    vc = vc_ref[...]
    kn = kn_ref[...]
    vn = vn_ref[...]
    lanes = lax.broadcasted_iota(jnp.int32, q.shape, 1)
    cache_cols = lax.broadcasted_iota(jnp.int32, (q.shape[0], kc.shape[0]), 1)
    cache_ok = cache_cols < cached
    new_cols = lax.broadcasted_iota(jnp.int32, (q.shape[0], kn.shape[0]), 1)
    new_rows = lax.broadcasted_iota(jnp.int32, (q.shape[0], kn.shape[0]), 0) + row0
    new_ok = (new_cols <= new_rows) & (new_cols < valid)
    scale = 1.0 / float(HD) ** 0.5
    dims = (((1,), (1,)), ((), ()))
    result = jnp.zeros(q.shape, jnp.float32)
    for head in range(2):
        mine = (lanes // HD) == head
        qh = jnp.where(mine, q, jnp.zeros_like(q))
        s_c = lax.dot_general(qh, kc, dims, preferred_element_type=jnp.float32) * scale
        s_n = lax.dot_general(qh, kn, dims, preferred_element_type=jnp.float32) * scale
        s_c = jnp.where(cache_ok, s_c, -jnp.inf)
        s_n = jnp.where(new_ok, s_n, -jnp.inf)
        peak = jnp.maximum(jnp.max(s_c, axis=1, keepdims=True), jnp.max(s_n, axis=1, keepdims=True))
        e_c = jnp.exp(s_c - peak)
        e_n = jnp.exp(s_n - peak)
        total = jnp.sum(e_c, axis=1, keepdims=True) + jnp.sum(e_n, axis=1, keepdims=True)
        mixed = jnp.dot(e_c.astype(jnp.bfloat16), vc, preferred_element_type=jnp.float32) + jnp.dot(
            e_n.astype(jnp.bfloat16), vn, preferred_element_type=jnp.float32
        )
        result = jnp.where(mine, mixed / total, result)
    out_ref[...] = result.astype(out_ref.dtype)


def attention(lens, queries, cache_k, cache_v, keys_new, values_new):
    rows, width = queries.shape
    cache_rows = cache_k.shape[0]
    pairs = width // PAIR
    chunks = rows // ROWS
    flops = 4 * rows * (cache_rows + rows) * width * 2
    return pl.pallas_call(
        attention_kernel,
        out_shape=jax.ShapeDtypeStruct((rows, width), jnp.bfloat16),
        grid_spec=pltpu.PrefetchScalarGridSpec(
            num_scalar_prefetch=1,
            grid=(pairs, chunks),
            in_specs=[
                pl.BlockSpec((ROWS, PAIR), lambda p, r, lens: (r, p)),
                pl.BlockSpec((cache_rows, PAIR), lambda p, r, lens: (0, p)),
                pl.BlockSpec((cache_rows, PAIR), lambda p, r, lens: (0, p)),
                pl.BlockSpec((rows, PAIR), lambda p, r, lens: (0, p)),
                pl.BlockSpec((rows, PAIR), lambda p, r, lens: (0, p)),
            ],
            out_specs=pl.BlockSpec((ROWS, PAIR), lambda p, r, lens: (r, p)),
        ),
        cost_estimate=pl.CostEstimate(
            flops=flops,
            transcendentals=rows * (cache_rows + rows) * width // HD,
            bytes_accessed=2 * (2 * rows * width + 2 * cache_rows * width + 2 * rows * width),
        ),
    )(lens, queries, cache_k, cache_v, keys_new, values_new)


HIDDEN_CHUNK = 256


def ffn_kernel(x_ref, wu_ref, wd_ref, out_ref, acc_ref):
    step = pl.program_id(0)

    @pl.when(step == 0)
    def _():
        acc_ref[...] = jnp.zeros_like(acc_ref)

    hidden = jnp.dot(x_ref[...], wu_ref[...], preferred_element_type=jnp.float32)
    active = (hidden * (0.5 + 0.5 * lax.erf(hidden * (0.5**0.5)))).astype(jnp.bfloat16)
    acc_ref[...] += jnp.dot(active, wd_ref[...], preferred_element_type=jnp.float32)

    @pl.when(step == pl.num_programs(0) - 1)
    def _():
        out_ref[...] = acc_ref[...].astype(out_ref.dtype)


def ffn(middle, w_up, w_down):
    rows, width = middle.shape
    hidden = w_up.shape[1]
    return pl.pallas_call(
        ffn_kernel,
        out_shape=jax.ShapeDtypeStruct((rows, width), jnp.bfloat16),
        grid=(hidden // HIDDEN_CHUNK,),
        in_specs=[
            pl.BlockSpec((rows, width), lambda c: (0, 0)),
            pl.BlockSpec((width, HIDDEN_CHUNK), lambda c: (0, c)),
            pl.BlockSpec((HIDDEN_CHUNK, width), lambda c: (c, 0)),
        ],
        out_specs=pl.BlockSpec((rows, width), lambda c: (0, 0)),
        scratch_shapes=[pltpu.VMEM((rows, width), jnp.float32)],
        cost_estimate=pl.CostEstimate(
            flops=4 * rows * width * hidden,
            transcendentals=rows * hidden,
            bytes_accessed=2 * (2 * rows * width + 2 * width * hidden),
        ),
    )(middle, w_up, w_down)


def finish_rows(attn_mixed, tokens, w_out, w_up, w_down, ln_gains, ln_biases):
    attn_sum = pair_sum(jnp.dot(attn_mixed, w_out, preferred_element_type=jnp.float32))
    middle = normalize(tokens.astype(jnp.float32) + attn_sum, ln_gains[0], ln_biases[0]).astype(
        jnp.bfloat16
    )
    ffn_sum = pair_sum(ffn(middle, w_up, w_down))
    return normalize(middle.astype(jnp.float32) + ffn_sum, ln_gains[1], ln_biases[1]).astype(
        jnp.bfloat16
    )


def shards(
    tokens,
    group_len,
    cache_len,
    cache_keys,
    cache_values,
    w_query,
    w_key,
    w_value,
    w_out,
    w_up,
    w_down,
    ln_gains,
    ln_biases,
    embed,
):
    block_rows = tokens.shape[0]
    local_width = w_query.shape[1]
    my_index = lax.axis_index("req")
    my_cache = lax.dynamic_index_in_dim(cache_len, my_index, 0, keepdims=False)
    my_valid = group_len[0]
    queries = jnp.dot(tokens, w_query, preferred_element_type=jnp.float32).astype(jnp.bfloat16)
    keys_new = jnp.dot(tokens, w_key, preferred_element_type=jnp.float32).astype(jnp.bfloat16)
    values_new = jnp.dot(tokens, w_value, preferred_element_type=jnp.float32).astype(jnp.bfloat16)
    lens = jnp.stack([my_cache, my_valid]).astype(jnp.int32)
    attn_mixed = attention(lens, queries, cache_keys[0], cache_values[0], keys_new, values_new)
    half = block_rows // 2
    layer_out = jnp.concatenate(
        [
            finish_rows(attn_mixed[:half], tokens[:half], w_out, w_up, w_down, ln_gains, ln_biases),
            finish_rows(attn_mixed[half:], tokens[half:], w_out, w_up, w_down, ln_gains, ln_biases),
        ],
        axis=0,
    )
    last_row = lax.dynamic_slice_in_dim(layer_out, my_valid - 1, 1, 0)
    reqs = cache_len.shape[0]
    all_rows = lax.all_to_all(
        jnp.broadcast_to(last_row, (reqs, last_row.shape[1])), "req", 0, 0, tiled=True
    )
    logits = jnp.einsum("rd,vd->rv", all_rows, embed, preferred_element_type=jnp.float32)
    slice_best = jnp.max(logits, axis=1)
    spread = jnp.repeat(slice_best, 2)[:, None]
    best_logit = jnp.max(lax.all_to_all(spread, ("req", "tp"), 0, 0, tiled=True), axis=0)
    return (layer_out, best_logit, slice_best[:, None])


def solution(mesh):
    placed = (
        P("req", None),
        P("req"),
        P(),
        P("req", None, "tp"),
        P("req", None, "tp"),
        P(None, "tp"),
        P(None, "tp"),
        P(None, "tp"),
        P("tp", None),
        P(None, "tp"),
        P("tp", None),
        P(),
        P(),
        P(("req", "tp"), None),
    )
    return jax.shard_map(
        shards,
        mesh=mesh,
        in_specs=placed,
        out_specs=(P("req", None), P("req"), P(None, ("req", "tp"))),
        check_vma=False,
    )
```

```python
import jax
import jax.numpy as jnp
from jax import lax
from jax.experimental import pallas as pl
from jax.experimental.pallas import tpu as pltpu
from jax.sharding import PartitionSpec as P

HD = 64


def normalize(rows, gain, bias):
    center = rows - jnp.mean(rows, axis=-1, keepdims=True)
    spread = jnp.mean(center * center, axis=-1, keepdims=True)
    return center * lax.rsqrt(spread + 1e-05) * gain + bias


def pair_sum(partial):
    own = partial.astype(jnp.bfloat16)
    other = lax.ppermute(own, "tp", [(0, 1), (1, 0)])
    return own.astype(jnp.float32) + other.astype(jnp.float32)


PAIR = 2 * HD
ROWS = 256


def attention_kernel(lens_ref, q_ref, kc_ref, vc_ref, kn_ref, vn_ref, out_ref):
    cached = lens_ref[0]
    valid = lens_ref[1]
    row0 = pl.program_id(1) * ROWS
    q = q_ref[...]
    kc = kc_ref[...]
    vc = vc_ref[...]
    kn = kn_ref[...]
    vn = vn_ref[...]
    lanes = lax.broadcasted_iota(jnp.int32, q.shape, 1)
    cache_cols = lax.broadcasted_iota(jnp.int32, (q.shape[0], kc.shape[0]), 1)
    cache_ok = cache_cols < cached
    new_cols = lax.broadcasted_iota(jnp.int32, (q.shape[0], kn.shape[0]), 1)
    new_rows = lax.broadcasted_iota(jnp.int32, (q.shape[0], kn.shape[0]), 0) + row0
    new_ok = (new_cols <= new_rows) & (new_cols < valid)
    scale = 1.0 / float(HD) ** 0.5
    dims = (((1,), (1,)), ((), ()))
    result = jnp.zeros(q.shape, jnp.float32)
    for head in range(2):
        mine = (lanes // HD) == head
        qh = jnp.where(mine, q, jnp.zeros_like(q))
        s_c = lax.dot_general(qh, kc, dims, preferred_element_type=jnp.float32) * scale
        s_n = lax.dot_general(qh, kn, dims, preferred_element_type=jnp.float32) * scale
        s_c = jnp.where(cache_ok, s_c, -jnp.inf)
        s_n = jnp.where(new_ok, s_n, -jnp.inf)
        peak = jnp.maximum(jnp.max(s_c, axis=1, keepdims=True), jnp.max(s_n, axis=1, keepdims=True))
        e_c = jnp.exp(s_c - peak)
        e_n = jnp.exp(s_n - peak)
        total = jnp.sum(e_c, axis=1, keepdims=True) + jnp.sum(e_n, axis=1, keepdims=True)
        mixed = jnp.dot(e_c.astype(jnp.bfloat16), vc, preferred_element_type=jnp.float32) + jnp.dot(
            e_n.astype(jnp.bfloat16), vn, preferred_element_type=jnp.float32
        )
        result = jnp.where(mine, mixed / total, result)
    out_ref[...] = result.astype(out_ref.dtype)


def attention(lens, queries, cache_k, cache_v, keys_new, values_new):
    rows, width = queries.shape
    cache_rows = cache_k.shape[0]
    pairs = width // PAIR
    chunks = rows // ROWS
    flops = 4 * rows * (cache_rows + rows) * width * 2
    return pl.pallas_call(
        attention_kernel,
        out_shape=jax.ShapeDtypeStruct((rows, width), jnp.bfloat16),
        grid_spec=pltpu.PrefetchScalarGridSpec(
            num_scalar_prefetch=1,
            grid=(pairs, chunks),
            in_specs=[
                pl.BlockSpec((ROWS, PAIR), lambda p, r, lens: (r, p)),
                pl.BlockSpec((cache_rows, PAIR), lambda p, r, lens: (0, p)),
                pl.BlockSpec((cache_rows, PAIR), lambda p, r, lens: (0, p)),
                pl.BlockSpec((rows, PAIR), lambda p, r, lens: (0, p)),
                pl.BlockSpec((rows, PAIR), lambda p, r, lens: (0, p)),
            ],
            out_specs=pl.BlockSpec((ROWS, PAIR), lambda p, r, lens: (r, p)),
        ),
        cost_estimate=pl.CostEstimate(
            flops=flops,
            transcendentals=rows * (cache_rows + rows) * width // HD,
            bytes_accessed=2 * (2 * rows * width + 2 * cache_rows * width + 2 * rows * width),
        ),
    )(lens, queries, cache_k, cache_v, keys_new, values_new)


def finish_rows(attn_mixed, tokens, w_out, w_up, w_down, ln_gains, ln_biases):
    attn_sum = pair_sum(jnp.dot(attn_mixed, w_out, preferred_element_type=jnp.float32))
    middle = normalize(tokens.astype(jnp.float32) + attn_sum, ln_gains[0], ln_biases[0]).astype(
        jnp.bfloat16
    )
    active = jax.nn.gelu(
        jnp.dot(middle, w_up, preferred_element_type=jnp.float32), approximate=False
    ).astype(jnp.bfloat16)
    ffn_sum = pair_sum(jnp.dot(active, w_down, preferred_element_type=jnp.float32))
    return normalize(middle.astype(jnp.float32) + ffn_sum, ln_gains[1], ln_biases[1]).astype(
        jnp.bfloat16
    )


def shards(
    tokens,
    group_len,
    cache_len,
    cache_keys,
    cache_values,
    w_query,
    w_key,
    w_value,
    w_out,
    w_up,
    w_down,
    ln_gains,
    ln_biases,
    embed,
):
    block_rows = tokens.shape[0]
    local_width = w_query.shape[1]
    my_index = lax.axis_index("req")
    my_cache = lax.dynamic_index_in_dim(cache_len, my_index, 0, keepdims=False)
    my_valid = group_len[0]
    queries = jnp.dot(tokens, w_query, preferred_element_type=jnp.float32).astype(jnp.bfloat16)
    keys_new = jnp.dot(tokens, w_key, preferred_element_type=jnp.float32).astype(jnp.bfloat16)
    values_new = jnp.dot(tokens, w_value, preferred_element_type=jnp.float32).astype(jnp.bfloat16)
    lens = jnp.stack([my_cache, my_valid]).astype(jnp.int32)
    attn_mixed = attention(lens, queries, cache_keys[0], cache_values[0], keys_new, values_new)
    half = block_rows // 2
    layer_out = jnp.concatenate(
        [
            finish_rows(attn_mixed[:half], tokens[:half], w_out, w_up, w_down, ln_gains, ln_biases),
            finish_rows(attn_mixed[half:], tokens[half:], w_out, w_up, w_down, ln_gains, ln_biases),
        ],
        axis=0,
    )
    last_row = lax.dynamic_slice_in_dim(layer_out, my_valid - 1, 1, 0)
    reqs = cache_len.shape[0]
    width = last_row.shape[1] // 2
    my_half = lax.dynamic_slice_in_dim(last_row, lax.axis_index("tp") * width, width, 1)
    all_rows = lax.all_to_all(
        jnp.broadcast_to(my_half, (2 * reqs, width)), ("req", "tp"), 0, 0, tiled=True
    ).reshape(reqs, 2 * width)
    logits = jnp.einsum("rd,vd->rv", all_rows, embed, preferred_element_type=jnp.float32)
    slice_best = jnp.max(logits, axis=1)
    spread = jnp.repeat(slice_best, 2)[:, None]
    best_logit = jnp.max(lax.all_to_all(spread, ("req", "tp"), 0, 0, tiled=True), axis=0)
    return (layer_out, best_logit, slice_best[:, None])


def solution(mesh):
    placed = (
        P("req", None),
        P("req"),
        P(),
        P("req", None, "tp"),
        P("req", None, "tp"),
        P(None, "tp"),
        P(None, "tp"),
        P(None, "tp"),
        P("tp", None),
        P(None, "tp"),
        P("tp", None),
        P(),
        P(),
        P(("req", "tp"), None),
    )
    return jax.shard_map(
        shards,
        mesh=mesh,
        in_specs=placed,
        out_specs=(P("req", None), P("req"), P(None, ("req", "tp"))),
        check_vma=False,
    )
```

```python
import jax
import jax.numpy as jnp
from jax import lax
from jax.experimental import pallas as pl
from jax.experimental.pallas import tpu as pltpu
from jax.sharding import PartitionSpec as P

HD = 64


def normalize(rows, gain, bias):
    center = rows - jnp.mean(rows, axis=-1, keepdims=True)
    spread = jnp.mean(center * center, axis=-1, keepdims=True)
    return center * lax.rsqrt(spread + 1e-05) * gain + bias


def pair_sum(partial):
    own = partial.astype(jnp.bfloat16)
    other = lax.ppermute(own, "tp", [(0, 1), (1, 0)])
    return own.astype(jnp.float32) + other.astype(jnp.float32)


PAIR = 2 * HD
ROWS = 256


def attention_kernel(lens_ref, q_ref, kc_ref, vc_ref, kn_ref, vn_ref, out_ref):
    cached = lens_ref[0]
    valid = lens_ref[1]
    row0 = pl.program_id(1) * ROWS
    q = q_ref[...]
    kc = kc_ref[...]
    vc = vc_ref[...]
    kn = kn_ref[...]
    vn = vn_ref[...]
    lanes = lax.broadcasted_iota(jnp.int32, q.shape, 1)
    cache_cols = lax.broadcasted_iota(jnp.int32, (q.shape[0], kc.shape[0]), 1)
    cache_ok = cache_cols < cached
    new_cols = lax.broadcasted_iota(jnp.int32, (q.shape[0], kn.shape[0]), 1)
    new_rows = lax.broadcasted_iota(jnp.int32, (q.shape[0], kn.shape[0]), 0) + row0
    new_ok = (new_cols <= new_rows) & (new_cols < valid)
    scale = 1.0 / float(HD) ** 0.5
    dims = (((1,), (1,)), ((), ()))
    result = jnp.zeros(q.shape, jnp.float32)
    for head in range(2):
        mine = (lanes // HD) == head
        qh = jnp.where(mine, q, jnp.zeros_like(q))
        s_c = lax.dot_general(qh, kc, dims, preferred_element_type=jnp.float32) * scale
        s_n = lax.dot_general(qh, kn, dims, preferred_element_type=jnp.float32) * scale
        s_c = jnp.where(cache_ok, s_c, -jnp.inf)
        s_n = jnp.where(new_ok, s_n, -jnp.inf)
        peak = jnp.maximum(jnp.max(s_c, axis=1, keepdims=True), jnp.max(s_n, axis=1, keepdims=True))
        e_c = jnp.exp(s_c - peak)
        e_n = jnp.exp(s_n - peak)
        total = jnp.sum(e_c, axis=1, keepdims=True) + jnp.sum(e_n, axis=1, keepdims=True)
        mixed = jnp.dot(e_c.astype(jnp.bfloat16), vc, preferred_element_type=jnp.float32) + jnp.dot(
            e_n.astype(jnp.bfloat16), vn, preferred_element_type=jnp.float32
        )
        result = jnp.where(mine, mixed / total, result)
    out_ref[...] = result.astype(out_ref.dtype)


def attention(lens, queries, cache_k, cache_v, keys_new, values_new):
    rows, width = queries.shape
    cache_rows = cache_k.shape[0]
    pairs = width // PAIR
    chunks = rows // ROWS
    flops = 4 * rows * (cache_rows + rows) * width * 2
    return pl.pallas_call(
        attention_kernel,
        out_shape=jax.ShapeDtypeStruct((rows, width), jnp.bfloat16),
        grid_spec=pltpu.PrefetchScalarGridSpec(
            num_scalar_prefetch=1,
            grid=(pairs, chunks),
            in_specs=[
                pl.BlockSpec((ROWS, PAIR), lambda p, r, lens: (r, p)),
                pl.BlockSpec((cache_rows, PAIR), lambda p, r, lens: (0, p)),
                pl.BlockSpec((cache_rows, PAIR), lambda p, r, lens: (0, p)),
                pl.BlockSpec((rows, PAIR), lambda p, r, lens: (0, p)),
                pl.BlockSpec((rows, PAIR), lambda p, r, lens: (0, p)),
            ],
            out_specs=pl.BlockSpec((ROWS, PAIR), lambda p, r, lens: (r, p)),
        ),
        cost_estimate=pl.CostEstimate(
            flops=flops,
            transcendentals=rows * (cache_rows + rows) * width // HD,
            bytes_accessed=2 * (2 * rows * width + 2 * cache_rows * width + 2 * rows * width),
        ),
    )(lens, queries, cache_k, cache_v, keys_new, values_new)


def shards(
    tokens,
    group_len,
    cache_len,
    cache_keys,
    cache_values,
    w_query,
    w_key,
    w_value,
    w_out,
    w_up,
    w_down,
    ln_gains,
    ln_biases,
    embed,
):
    xy_size = lax.psum(1, "xy")
    z_size = lax.psum(1, "z")
    tp_size = lax.psum(1, "tp")
    block_rows = tokens.shape[0]
    local_width = w_query.shape[1]
    my_index = lax.axis_index(("xy", "z"))
    my_cache = lax.dynamic_index_in_dim(cache_len, my_index, 0, keepdims=False)
    my_valid = group_len[0]
    queries = jnp.dot(tokens, w_query, preferred_element_type=jnp.float32).astype(jnp.bfloat16)
    keys_new = jnp.dot(tokens, w_key, preferred_element_type=jnp.float32).astype(jnp.bfloat16)
    values_new = jnp.dot(tokens, w_value, preferred_element_type=jnp.float32).astype(jnp.bfloat16)
    lens = jnp.stack([my_cache, my_valid]).astype(jnp.int32)
    attn_mixed = attention(lens, queries, cache_keys[0], cache_values[0], keys_new, values_new)
    attn_sum = pair_sum(jnp.dot(attn_mixed, w_out, preferred_element_type=jnp.float32))
    middle = normalize(tokens.astype(jnp.float32) + attn_sum, ln_gains[0], ln_biases[0]).astype(
        jnp.bfloat16
    )
    active = jax.nn.gelu(
        jnp.dot(middle, w_up, preferred_element_type=jnp.float32), approximate=False
    ).astype(jnp.bfloat16)
    ffn_sum = pair_sum(jnp.dot(active, w_down, preferred_element_type=jnp.float32))
    layer_out = normalize(middle.astype(jnp.float32) + ffn_sum, ln_gains[1], ln_biases[1]).astype(
        jnp.bfloat16
    )
    last_row = lax.dynamic_slice_in_dim(layer_out, my_valid - 1, 1, 0)
    width = last_row.shape[1]
    near = lax.all_to_all(jnp.broadcast_to(last_row, (z_size, width)), "z", 0, 0, tiled=True)
    all_rows = lax.all_to_all(
        jnp.broadcast_to(near[None], (xy_size, z_size, width)), "xy", 0, 0, tiled=True
    ).reshape(xy_size * z_size, width)
    logits = jnp.einsum("rd,vd->rv", all_rows, embed, preferred_element_type=jnp.float32)
    slice_best = jnp.max(logits, axis=1)
    by_plane = lax.all_to_all(slice_best.reshape(xy_size, z_size), "xy", 0, 0, tiled=True)
    plane_best = jnp.max(by_plane, axis=0)
    spread = jnp.repeat(plane_best, tp_size)[:, None]
    best_logit = jnp.max(lax.all_to_all(spread, ("z", "tp"), 0, 0, tiled=True), axis=0)
    return (layer_out, best_logit, slice_best[:, None])


def z_extent(mesh):
    devices = mesh.devices.reshape(-1)
    coords = getattr(devices[0], "coords", None)
    if coords is None:
        return 8
    return len({tuple(d.coords)[2] for d in devices})


def solution(mesh):
    reqs, cores = mesh.devices.shape
    z = z_extent(mesh)
    fine = jax.sharding.Mesh(mesh.devices.reshape(reqs // z, z, cores), ("xy", "z", "tp"))
    R = ("xy", "z")
    placed = (
        P(R, None),
        P(R),
        P(),
        P(R, None, "tp"),
        P(R, None, "tp"),
        P(None, "tp"),
        P(None, "tp"),
        P(None, "tp"),
        P("tp", None),
        P(None, "tp"),
        P("tp", None),
        P(),
        P(),
        P(("xy", "z", "tp"), None),
    )
    return jax.shard_map(
        shards,
        mesh=fine,
        in_specs=placed,
        out_specs=(P(R, None), P(R), P(None, ("xy", "z", "tp"))),
        check_vma=False,
    )
```

```python
import jax
import jax.numpy as jnp
from jax import lax
from jax.experimental import pallas as pl
from jax.experimental.pallas import tpu as pltpu
from jax.sharding import PartitionSpec as P

HD = 64


def normalize(rows, gain, bias):
    center = rows - jnp.mean(rows, axis=-1, keepdims=True)
    spread = jnp.mean(center * center, axis=-1, keepdims=True)
    return center * lax.rsqrt(spread + 1e-05) * gain + bias


def pair_sum(partial):
    own = partial.astype(jnp.bfloat16)
    other = lax.ppermute(own, "tp", [(0, 1), (1, 0)])
    return own.astype(jnp.float32) + other.astype(jnp.float32)


PAIR = 2 * HD
ROWS = 256


def attention_kernel(lens_ref, q_ref, kc_ref, vc_ref, kn_ref, vn_ref, out_ref):
    cached = lens_ref[0]
    valid = lens_ref[1]
    row0 = pl.program_id(1) * ROWS
    q = q_ref[...]
    kc = kc_ref[...]
    vc = vc_ref[...]
    kn = kn_ref[...]
    vn = vn_ref[...]
    lanes = lax.broadcasted_iota(jnp.int32, q.shape, 1)
    cache_cols = lax.broadcasted_iota(jnp.int32, (q.shape[0], kc.shape[0]), 1)
    cache_ok = cache_cols < cached
    new_cols = lax.broadcasted_iota(jnp.int32, (q.shape[0], kn.shape[0]), 1)
    new_rows = lax.broadcasted_iota(jnp.int32, (q.shape[0], kn.shape[0]), 0) + row0
    new_ok = (new_cols <= new_rows) & (new_cols < valid)
    scale = 1.0 / float(HD) ** 0.5
    dims = (((1,), (1,)), ((), ()))
    result = jnp.zeros(q.shape, jnp.float32)
    for head in range(2):
        mine = (lanes // HD) == head
        qh = jnp.where(mine, q, jnp.zeros_like(q))
        s_c = lax.dot_general(qh, kc, dims, preferred_element_type=jnp.float32) * scale
        s_n = lax.dot_general(qh, kn, dims, preferred_element_type=jnp.float32) * scale
        s_c = jnp.where(cache_ok, s_c, -jnp.inf)
        s_n = jnp.where(new_ok, s_n, -jnp.inf)
        peak = jnp.maximum(jnp.max(s_c, axis=1, keepdims=True), jnp.max(s_n, axis=1, keepdims=True))
        e_c = jnp.exp(s_c - peak)
        e_n = jnp.exp(s_n - peak)
        total = jnp.sum(e_c, axis=1, keepdims=True) + jnp.sum(e_n, axis=1, keepdims=True)
        mixed = jnp.dot(e_c.astype(jnp.bfloat16), vc, preferred_element_type=jnp.float32) + jnp.dot(
            e_n.astype(jnp.bfloat16), vn, preferred_element_type=jnp.float32
        )
        result = jnp.where(mine, mixed / total, result)
    out_ref[...] = result.astype(out_ref.dtype)


def attention(lens, queries, cache_k, cache_v, keys_new, values_new):
    rows, width = queries.shape
    cache_rows = cache_k.shape[0]
    pairs = width // PAIR
    chunks = rows // ROWS
    flops = 4 * rows * (cache_rows + rows) * width * 2
    return pl.pallas_call(
        attention_kernel,
        out_shape=jax.ShapeDtypeStruct((rows, width), jnp.bfloat16),
        grid_spec=pltpu.PrefetchScalarGridSpec(
            num_scalar_prefetch=1,
            grid=(pairs, chunks),
            in_specs=[
                pl.BlockSpec((ROWS, PAIR), lambda p, r, lens: (r, p)),
                pl.BlockSpec((cache_rows, PAIR), lambda p, r, lens: (0, p)),
                pl.BlockSpec((cache_rows, PAIR), lambda p, r, lens: (0, p)),
                pl.BlockSpec((rows, PAIR), lambda p, r, lens: (0, p)),
                pl.BlockSpec((rows, PAIR), lambda p, r, lens: (0, p)),
            ],
            out_specs=pl.BlockSpec((ROWS, PAIR), lambda p, r, lens: (r, p)),
        ),
        cost_estimate=pl.CostEstimate(
            flops=flops,
            transcendentals=rows * (cache_rows + rows) * width // HD,
            bytes_accessed=2 * (2 * rows * width + 2 * cache_rows * width + 2 * rows * width),
        ),
    )(lens, queries, cache_k, cache_v, keys_new, values_new)


def shards(
    tokens,
    group_len,
    cache_len,
    cache_keys,
    cache_values,
    w_query,
    w_key,
    w_value,
    w_out,
    w_up,
    w_down,
    ln_gains,
    ln_biases,
    embed,
):
    block_rows = tokens.shape[0]
    local_width = w_query.shape[1]
    my_index = lax.axis_index("req")
    my_cache = lax.dynamic_index_in_dim(cache_len, my_index, 0, keepdims=False)
    my_valid = group_len[0]
    queries = jnp.dot(tokens, w_query, preferred_element_type=jnp.float32).astype(jnp.bfloat16)
    keys_new = jnp.dot(tokens, w_key, preferred_element_type=jnp.float32).astype(jnp.bfloat16)
    values_new = jnp.dot(tokens, w_value, preferred_element_type=jnp.float32).astype(jnp.bfloat16)
    lens = jnp.stack([my_cache, my_valid]).astype(jnp.int32)
    attn_mixed = attention(lens, queries, cache_keys[0], cache_values[0], keys_new, values_new)
    attn_sum = pair_sum(jnp.dot(attn_mixed, w_out, preferred_element_type=jnp.float32))
    middle = normalize(tokens.astype(jnp.float32) + attn_sum, ln_gains[0], ln_biases[0]).astype(
        jnp.bfloat16
    )
    active = jax.nn.gelu(
        jnp.dot(middle, w_up, preferred_element_type=jnp.float32), approximate=False
    ).astype(jnp.bfloat16)
    ffn_sum = pair_sum(jnp.dot(active, w_down, preferred_element_type=jnp.float32))
    layer_out = normalize(middle.astype(jnp.float32) + ffn_sum, ln_gains[1], ln_biases[1]).astype(
        jnp.bfloat16
    )
    last_row = lax.dynamic_slice_in_dim(layer_out, my_valid - 1, 1, 0)
    reqs = cache_len.shape[0]
    all_rows = lax.all_to_all(
        jnp.broadcast_to(last_row, (reqs, last_row.shape[1])), "req", 0, 0, tiled=True
    )
    logits = jnp.einsum("rd,vd->rv", all_rows, embed, preferred_element_type=jnp.float32)
    slice_best = jnp.max(logits, axis=1)
    spread = jnp.repeat(slice_best, 2)[:, None]
    best_logit = jnp.max(lax.all_to_all(spread, ("req", "tp"), 0, 0, tiled=True), axis=0)
    return (layer_out, best_logit, slice_best[:, None])


def solution(mesh):
    placed = (
        P("req", None),
        P("req"),
        P(),
        P("req", None, "tp"),
        P("req", None, "tp"),
        P(None, "tp"),
        P(None, "tp"),
        P(None, "tp"),
        P("tp", None),
        P(None, "tp"),
        P("tp", None),
        P(),
        P(),
        P(("req", "tp"), None),
    )
    return jax.shard_map(
        shards,
        mesh=mesh,
        in_specs=placed,
        out_specs=(P("req", None), P("req"), P(None, ("req", "tp"))),
        check_vma=False,
    )
```

```python
import jax
import jax.numpy as jnp
from jax import lax
from jax.experimental import pallas as pl
from jax.experimental.pallas import tpu as pltpu
from jax.sharding import PartitionSpec as P

HD = 64


def normalize(rows, gain, bias):
    center = rows - jnp.mean(rows, axis=-1, keepdims=True)
    spread = jnp.mean(center * center, axis=-1, keepdims=True)
    return center * lax.rsqrt(spread + 1e-05) * gain + bias


def pair_sum(partial):
    own = partial.astype(jnp.bfloat16)
    other = lax.ppermute(own, "tp", [(0, 1), (1, 0)])
    return own.astype(jnp.float32) + other.astype(jnp.float32)


PAIR = 2 * HD
ROWS = 256


def attention_kernel(lens_ref, x_ref, wq_ref, wk_ref, wv_ref, kc_ref, vc_ref, out_ref):
    cached = lens_ref[0]
    valid = lens_ref[1]
    x = x_ref[...]
    q_all = jnp.dot(x, wq_ref[...], preferred_element_type=jnp.float32).astype(jnp.bfloat16)
    kn = jnp.dot(x, wk_ref[...], preferred_element_type=jnp.float32).astype(jnp.bfloat16)
    vn = jnp.dot(x, wv_ref[...], preferred_element_type=jnp.float32).astype(jnp.bfloat16)
    kc = kc_ref[...]
    vc = vc_ref[...]
    scale = 1.0 / float(HD) ** 0.5
    dims = (((1,), (1,)), ((), ()))
    for chunk in range(x.shape[0] // ROWS):
        row0 = chunk * ROWS
        q = q_all[row0 : row0 + ROWS]
        lanes = lax.broadcasted_iota(jnp.int32, q.shape, 1)
        cache_cols = lax.broadcasted_iota(jnp.int32, (ROWS, kc.shape[0]), 1)
        cache_ok = cache_cols < cached
        new_cols = lax.broadcasted_iota(jnp.int32, (ROWS, kn.shape[0]), 1)
        new_rows = lax.broadcasted_iota(jnp.int32, (ROWS, kn.shape[0]), 0) + row0
        new_ok = (new_cols <= new_rows) & (new_cols < valid)
        result = jnp.zeros(q.shape, jnp.float32)
        for head in range(2):
            mine = (lanes // HD) == head
            qh = jnp.where(mine, q, jnp.zeros_like(q))
            s_c = lax.dot_general(qh, kc, dims, preferred_element_type=jnp.float32) * scale
            s_n = lax.dot_general(qh, kn, dims, preferred_element_type=jnp.float32) * scale
            s_c = jnp.where(cache_ok, s_c, -jnp.inf)
            s_n = jnp.where(new_ok, s_n, -jnp.inf)
            peak = jnp.maximum(
                jnp.max(s_c, axis=1, keepdims=True), jnp.max(s_n, axis=1, keepdims=True)
            )
            e_c = jnp.exp(s_c - peak)
            e_n = jnp.exp(s_n - peak)
            total = jnp.sum(e_c, axis=1, keepdims=True) + jnp.sum(e_n, axis=1, keepdims=True)
            mixed = jnp.dot(
                e_c.astype(jnp.bfloat16), vc, preferred_element_type=jnp.float32
            ) + jnp.dot(e_n.astype(jnp.bfloat16), vn, preferred_element_type=jnp.float32)
            result = jnp.where(mine, mixed / total, result)
        out_ref[row0 : row0 + ROWS, :] = result.astype(out_ref.dtype)


def attention(lens, tokens, w_query, w_key, w_value, cache_k, cache_v):
    rows, model = tokens.shape
    width = w_query.shape[1]
    cache_rows = cache_k.shape[0]
    pairs = width // PAIR
    flops = 4 * rows * (cache_rows + rows) * width * 2 + 6 * rows * model * width
    return pl.pallas_call(
        attention_kernel,
        out_shape=jax.ShapeDtypeStruct((rows, width), jnp.bfloat16),
        grid_spec=pltpu.PrefetchScalarGridSpec(
            num_scalar_prefetch=1,
            grid=(pairs,),
            in_specs=[
                pl.BlockSpec((rows, model), lambda p, lens: (0, 0)),
                pl.BlockSpec((model, PAIR), lambda p, lens: (0, p)),
                pl.BlockSpec((model, PAIR), lambda p, lens: (0, p)),
                pl.BlockSpec((model, PAIR), lambda p, lens: (0, p)),
                pl.BlockSpec((cache_rows, PAIR), lambda p, lens: (0, p)),
                pl.BlockSpec((cache_rows, PAIR), lambda p, lens: (0, p)),
            ],
            out_specs=pl.BlockSpec((rows, PAIR), lambda p, lens: (0, p)),
        ),
        cost_estimate=pl.CostEstimate(
            flops=flops,
            transcendentals=rows * (cache_rows + rows) * width // HD,
            bytes_accessed=2 * (rows * model + 3 * model * width + 2 * cache_rows * width + rows * width),
        ),
    )(lens, tokens, w_query, w_key, w_value, cache_k, cache_v)


def shards(
    tokens,
    group_len,
    cache_len,
    cache_keys,
    cache_values,
    w_query,
    w_key,
    w_value,
    w_out,
    w_up,
    w_down,
    ln_gains,
    ln_biases,
    embed,
):
    block_rows = tokens.shape[0]
    local_width = w_query.shape[1]
    my_index = lax.axis_index("req")
    my_cache = lax.dynamic_index_in_dim(cache_len, my_index, 0, keepdims=False)
    my_valid = group_len[0]
    lens = jnp.stack([my_cache, my_valid]).astype(jnp.int32)
    attn_mixed = attention(lens, tokens, w_query, w_key, w_value, cache_keys[0], cache_values[0])
    attn_sum = pair_sum(jnp.dot(attn_mixed, w_out, preferred_element_type=jnp.float32))
    middle = normalize(tokens.astype(jnp.float32) + attn_sum, ln_gains[0], ln_biases[0]).astype(
        jnp.bfloat16
    )
    active = jax.nn.gelu(
        jnp.dot(middle, w_up, preferred_element_type=jnp.float32), approximate=False
    ).astype(jnp.bfloat16)
    ffn_sum = pair_sum(jnp.dot(active, w_down, preferred_element_type=jnp.float32))
    layer_out = normalize(middle.astype(jnp.float32) + ffn_sum, ln_gains[1], ln_biases[1]).astype(
        jnp.bfloat16
    )
    last_row = lax.dynamic_slice_in_dim(layer_out, my_valid - 1, 1, 0)
    reqs = cache_len.shape[0]
    all_rows = lax.all_to_all(
        jnp.broadcast_to(last_row, (reqs, last_row.shape[1])), "req", 0, 0, tiled=True
    )
    logits = jnp.einsum("rd,vd->rv", all_rows, embed, preferred_element_type=jnp.float32)
    slice_best = jnp.max(logits, axis=1)
    spread = jnp.repeat(slice_best, 2)[:, None]
    best_logit = jnp.max(lax.all_to_all(spread, ("req", "tp"), 0, 0, tiled=True), axis=0)
    return (layer_out, best_logit, slice_best[:, None])


def solution(mesh):
    placed = (
        P("req", None),
        P("req"),
        P(),
        P("req", None, "tp"),
        P("req", None, "tp"),
        P(None, "tp"),
        P(None, "tp"),
        P(None, "tp"),
        P("tp", None),
        P(None, "tp"),
        P("tp", None),
        P(),
        P(),
        P(("req", "tp"), None),
    )
    return jax.shard_map(
        shards,
        mesh=mesh,
        in_specs=placed,
        out_specs=(P("req", None), P("req"), P(None, ("req", "tp"))),
        check_vma=False,
    )
```

```python
import jax
import jax.numpy as jnp
from jax import lax
from jax.experimental import pallas as pl
from jax.experimental.pallas import tpu as pltpu
from jax.sharding import PartitionSpec as P

HD = 64


def normalize(rows, gain, bias):
    center = rows - jnp.mean(rows, axis=-1, keepdims=True)
    spread = jnp.mean(center * center, axis=-1, keepdims=True)
    return center * lax.rsqrt(spread + 1e-05) * gain + bias


def pair_sum(partial):
    own = partial.astype(jnp.bfloat16)
    other = lax.ppermute(own, "tp", [(0, 1), (1, 0)])
    return own.astype(jnp.float32) + other.astype(jnp.float32)


PAIR = 2 * HD
ROWS = 256


def attention_kernel(lens_ref, x_ref, wq_ref, wk_ref, wv_ref, kc_ref, vc_ref, out_ref):
    cached = lens_ref[0]
    valid = lens_ref[1]
    x = x_ref[...]
    q_all = jnp.dot(x, wq_ref[...], preferred_element_type=jnp.float32).astype(jnp.bfloat16)
    kn = jnp.dot(x, wk_ref[...], preferred_element_type=jnp.float32).astype(jnp.bfloat16)
    vn = jnp.dot(x, wv_ref[...], preferred_element_type=jnp.float32).astype(jnp.bfloat16)
    kc = kc_ref[...]
    vc = vc_ref[...]
    scale = 1.0 / float(HD) ** 0.5
    dims = (((1,), (1,)), ((), ()))
    for chunk in range(x.shape[0] // ROWS):
        row0 = chunk * ROWS
        q = q_all[row0 : row0 + ROWS]
        reach = row0 + ROWS
        kn_seen = kn[:reach]
        vn_seen = vn[:reach]
        lanes = lax.broadcasted_iota(jnp.int32, q.shape, 1)
        cache_cols = lax.broadcasted_iota(jnp.int32, (ROWS, kc.shape[0]), 1)
        cache_ok = cache_cols < cached
        new_cols = lax.broadcasted_iota(jnp.int32, (ROWS, reach), 1)
        new_rows = lax.broadcasted_iota(jnp.int32, (ROWS, reach), 0) + row0
        new_ok = (new_cols <= new_rows) & (new_cols < valid)
        result = jnp.zeros(q.shape, jnp.float32)
        for head in range(2):
            mine = (lanes // HD) == head
            qh = jnp.where(mine, q, jnp.zeros_like(q))
            s_c = lax.dot_general(qh, kc, dims, preferred_element_type=jnp.float32) * scale
            s_n = lax.dot_general(qh, kn_seen, dims, preferred_element_type=jnp.float32) * scale
            s_c = jnp.where(cache_ok, s_c, -jnp.inf)
            s_n = jnp.where(new_ok, s_n, -jnp.inf)
            peak = jnp.maximum(
                jnp.max(s_c, axis=1, keepdims=True), jnp.max(s_n, axis=1, keepdims=True)
            )
            e_c = jnp.exp(s_c - peak)
            e_n = jnp.exp(s_n - peak)
            total = jnp.sum(e_c, axis=1, keepdims=True) + jnp.sum(e_n, axis=1, keepdims=True)
            mixed = jnp.dot(
                e_c.astype(jnp.bfloat16), vc, preferred_element_type=jnp.float32
            ) + jnp.dot(e_n.astype(jnp.bfloat16), vn_seen, preferred_element_type=jnp.float32)
            result = jnp.where(mine, mixed / total, result)
        out_ref[row0 : row0 + ROWS, :] = result.astype(out_ref.dtype)


def attention(lens, tokens, w_query, w_key, w_value, cache_k, cache_v):
    rows, model = tokens.shape
    width = w_query.shape[1]
    cache_rows = cache_k.shape[0]
    pairs = width // PAIR
    flops = 4 * rows * (cache_rows + rows) * width * 2 + 6 * rows * model * width
    return pl.pallas_call(
        attention_kernel,
        out_shape=jax.ShapeDtypeStruct((rows, width), jnp.bfloat16),
        grid_spec=pltpu.PrefetchScalarGridSpec(
            num_scalar_prefetch=1,
            grid=(pairs,),
            in_specs=[
                pl.BlockSpec((rows, model), lambda p, lens: (0, 0)),
                pl.BlockSpec((model, PAIR), lambda p, lens: (0, p)),
                pl.BlockSpec((model, PAIR), lambda p, lens: (0, p)),
                pl.BlockSpec((model, PAIR), lambda p, lens: (0, p)),
                pl.BlockSpec((cache_rows, PAIR), lambda p, lens: (0, p)),
                pl.BlockSpec((cache_rows, PAIR), lambda p, lens: (0, p)),
            ],
            out_specs=pl.BlockSpec((rows, PAIR), lambda p, lens: (0, p)),
        ),
        cost_estimate=pl.CostEstimate(
            flops=flops,
            transcendentals=rows * (cache_rows + rows) * width // HD,
            bytes_accessed=2 * (rows * model + 3 * model * width + 2 * cache_rows * width + rows * width),
        ),
    )(lens, tokens, w_query, w_key, w_value, cache_k, cache_v)


def shards(
    tokens,
    group_len,
    cache_len,
    cache_keys,
    cache_values,
    w_query,
    w_key,
    w_value,
    w_out,
    w_up,
    w_down,
    ln_gains,
    ln_biases,
    embed,
):
    block_rows = tokens.shape[0]
    local_width = w_query.shape[1]
    my_index = lax.axis_index("req")
    my_cache = lax.dynamic_index_in_dim(cache_len, my_index, 0, keepdims=False)
    my_valid = group_len[0]
    lens = jnp.stack([my_cache, my_valid]).astype(jnp.int32)
    attn_mixed = attention(lens, tokens, w_query, w_key, w_value, cache_keys[0], cache_values[0])
    attn_sum = pair_sum(jnp.dot(attn_mixed, w_out, preferred_element_type=jnp.float32))
    middle = normalize(tokens.astype(jnp.float32) + attn_sum, ln_gains[0], ln_biases[0]).astype(
        jnp.bfloat16
    )
    active = jax.nn.gelu(
        jnp.dot(middle, w_up, preferred_element_type=jnp.float32), approximate=False
    ).astype(jnp.bfloat16)
    ffn_sum = pair_sum(jnp.dot(active, w_down, preferred_element_type=jnp.float32))
    layer_out = normalize(middle.astype(jnp.float32) + ffn_sum, ln_gains[1], ln_biases[1]).astype(
        jnp.bfloat16
    )
    last_row = lax.dynamic_slice_in_dim(layer_out, my_valid - 1, 1, 0)
    reqs = cache_len.shape[0]
    all_rows = lax.all_to_all(
        jnp.broadcast_to(last_row, (reqs, last_row.shape[1])), "req", 0, 0, tiled=True
    )
    logits = jnp.einsum("rd,vd->rv", all_rows, embed, preferred_element_type=jnp.float32)
    slice_best = jnp.max(logits, axis=1)
    spread = jnp.repeat(slice_best, 2)[:, None]
    best_logit = jnp.max(lax.all_to_all(spread, ("req", "tp"), 0, 0, tiled=True), axis=0)
    return (layer_out, best_logit, slice_best[:, None])


def solution(mesh):
    placed = (
        P("req", None),
        P("req"),
        P(),
        P("req", None, "tp"),
        P("req", None, "tp"),
        P(None, "tp"),
        P(None, "tp"),
        P(None, "tp"),
        P("tp", None),
        P(None, "tp"),
        P("tp", None),
        P(),
        P(),
        P(("req", "tp"), None),
    )
    return jax.shard_map(
        shards,
        mesh=mesh,
        in_specs=placed,
        out_specs=(P("req", None), P("req"), P(None, ("req", "tp"))),
        check_vma=False,
    )
```

```python
import jax
import jax.numpy as jnp
from jax import lax
from jax.experimental import pallas as pl
from jax.experimental.pallas import tpu as pltpu
from jax.sharding import PartitionSpec as P

HD = 64


def normalize(rows, gain, bias):
    center = rows - jnp.mean(rows, axis=-1, keepdims=True)
    spread = jnp.mean(center * center, axis=-1, keepdims=True)
    return center * lax.rsqrt(spread + 1e-05) * gain + bias


def pair_sum(partial):
    own = partial.astype(jnp.bfloat16)
    other = lax.ppermute(own, "tp", [(0, 1), (1, 0)])
    return own.astype(jnp.float32) + other.astype(jnp.float32)


PAIR = 2 * HD
ROWS = 256


def attention_kernel(cache_len_ref, group_len_ref, x_ref, wq_ref, wk_ref, wv_ref, kc_ref, vc_ref, out_ref):
    cached = cache_len_ref[lax.axis_index("req")]
    valid = group_len_ref[0]
    x = x_ref[...]
    q_all = jnp.dot(x, wq_ref[...], preferred_element_type=jnp.float32).astype(jnp.bfloat16)
    kn = jnp.dot(x, wk_ref[...], preferred_element_type=jnp.float32).astype(jnp.bfloat16)
    vn = jnp.dot(x, wv_ref[...], preferred_element_type=jnp.float32).astype(jnp.bfloat16)
    kc = kc_ref[...]
    vc = vc_ref[...]
    scale = 1.0 / float(HD) ** 0.5
    dims = (((1,), (1,)), ((), ()))
    for chunk in range(x.shape[0] // ROWS):
        row0 = chunk * ROWS
        q = q_all[row0 : row0 + ROWS]
        reach = row0 + ROWS
        kn_seen = kn[:reach]
        vn_seen = vn[:reach]
        lanes = lax.broadcasted_iota(jnp.int32, q.shape, 1)
        cache_cols = lax.broadcasted_iota(jnp.int32, (ROWS, kc.shape[0]), 1)
        cache_ok = cache_cols < cached
        new_cols = lax.broadcasted_iota(jnp.int32, (ROWS, reach), 1)
        new_rows = lax.broadcasted_iota(jnp.int32, (ROWS, reach), 0) + row0
        new_ok = (new_cols <= new_rows) & (new_cols < valid)
        result = jnp.zeros(q.shape, jnp.float32)
        for head in range(2):
            mine = (lanes // HD) == head
            qh = jnp.where(mine, q, jnp.zeros_like(q))
            s_c = lax.dot_general(qh, kc, dims, preferred_element_type=jnp.float32) * scale
            s_n = lax.dot_general(qh, kn_seen, dims, preferred_element_type=jnp.float32) * scale
            s_c = jnp.where(cache_ok, s_c, -jnp.inf)
            s_n = jnp.where(new_ok, s_n, -jnp.inf)
            peak = jnp.maximum(
                jnp.max(s_c, axis=1, keepdims=True), jnp.max(s_n, axis=1, keepdims=True)
            )
            e_c = jnp.exp(s_c - peak)
            e_n = jnp.exp(s_n - peak)
            total = jnp.sum(e_c, axis=1, keepdims=True) + jnp.sum(e_n, axis=1, keepdims=True)
            mixed = jnp.dot(
                e_c.astype(jnp.bfloat16), vc, preferred_element_type=jnp.float32
            ) + jnp.dot(e_n.astype(jnp.bfloat16), vn_seen, preferred_element_type=jnp.float32)
            result = jnp.where(mine, mixed / total, result)
        out_ref[row0 : row0 + ROWS, :] = result.astype(out_ref.dtype)


def attention(cache_len, group_len, tokens, w_query, w_key, w_value, cache_k, cache_v):
    rows, model = tokens.shape
    width = w_query.shape[1]
    cache_rows = cache_k.shape[0]
    pairs = width // PAIR
    flops = 4 * rows * (cache_rows + rows) * width * 2 + 6 * rows * model * width
    return pl.pallas_call(
        attention_kernel,
        out_shape=jax.ShapeDtypeStruct((rows, width), jnp.bfloat16),
        grid_spec=pltpu.PrefetchScalarGridSpec(
            num_scalar_prefetch=2,
            grid=(pairs,),
            in_specs=[
                pl.BlockSpec((rows, model), lambda p, c, g: (0, 0)),
                pl.BlockSpec((model, PAIR), lambda p, c, g: (0, p)),
                pl.BlockSpec((model, PAIR), lambda p, c, g: (0, p)),
                pl.BlockSpec((model, PAIR), lambda p, c, g: (0, p)),
                pl.BlockSpec((cache_rows, PAIR), lambda p, c, g: (0, p)),
                pl.BlockSpec((cache_rows, PAIR), lambda p, c, g: (0, p)),
            ],
            out_specs=pl.BlockSpec((rows, PAIR), lambda p, c, g: (0, p)),
        ),
        cost_estimate=pl.CostEstimate(
            flops=flops,
            transcendentals=rows * (cache_rows + rows) * width // HD,
            bytes_accessed=2 * (rows * model + 3 * model * width + 2 * cache_rows * width + rows * width),
        ),
    )(cache_len, group_len, tokens, w_query, w_key, w_value, cache_k, cache_v)


def shards(
    tokens,
    group_len,
    cache_len,
    cache_keys,
    cache_values,
    w_query,
    w_key,
    w_value,
    w_out,
    w_up,
    w_down,
    ln_gains,
    ln_biases,
    embed,
):
    block_rows = tokens.shape[0]
    local_width = w_query.shape[1]
    my_index = lax.axis_index("req")
    my_valid = group_len[0]
    attn_mixed = attention(cache_len, group_len, tokens, w_query, w_key, w_value, cache_keys[0], cache_values[0])
    attn_sum = pair_sum(jnp.dot(attn_mixed, w_out, preferred_element_type=jnp.float32))
    middle = normalize(tokens.astype(jnp.float32) + attn_sum, ln_gains[0], ln_biases[0]).astype(
        jnp.bfloat16
    )
    active = jax.nn.gelu(
        jnp.dot(middle, w_up, preferred_element_type=jnp.float32), approximate=False
    ).astype(jnp.bfloat16)
    ffn_sum = pair_sum(jnp.dot(active, w_down, preferred_element_type=jnp.float32))
    layer_out = normalize(middle.astype(jnp.float32) + ffn_sum, ln_gains[1], ln_biases[1]).astype(
        jnp.bfloat16
    )
    last_row = lax.dynamic_slice_in_dim(layer_out, my_valid - 1, 1, 0)
    reqs = cache_len.shape[0]
    all_rows = lax.all_to_all(
        jnp.broadcast_to(last_row, (reqs, last_row.shape[1])), "req", 0, 0, tiled=True
    )
    logits = jnp.einsum("rd,vd->rv", all_rows, embed, preferred_element_type=jnp.float32)
    slice_best = jnp.max(logits, axis=1)
    spread = jnp.repeat(slice_best, 2)[:, None]
    best_logit = jnp.max(lax.all_to_all(spread, ("req", "tp"), 0, 0, tiled=True), axis=0)
    return (layer_out, best_logit, slice_best[:, None])


def solution(mesh):
    placed = (
        P("req", None),
        P("req"),
        P(),
        P("req", None, "tp"),
        P("req", None, "tp"),
        P(None, "tp"),
        P(None, "tp"),
        P(None, "tp"),
        P("tp", None),
        P(None, "tp"),
        P("tp", None),
        P(),
        P(),
        P(("req", "tp"), None),
    )
    return jax.shard_map(
        shards,
        mesh=mesh,
        in_specs=placed,
        out_specs=(P("req", None), P("req"), P(None, ("req", "tp"))),
        check_vma=False,
    )
```

```python
import jax
import jax.numpy as jnp
from jax import lax
from jax.experimental import pallas as pl
from jax.experimental.pallas import tpu as pltpu
from jax.sharding import PartitionSpec as P

HD = 64


def normalize(rows, gain, bias):
    center = rows - jnp.mean(rows, axis=-1, keepdims=True)
    spread = jnp.mean(center * center, axis=-1, keepdims=True)
    return center * lax.rsqrt(spread + 1e-05) * gain + bias


def pair_sum(partial):
    own = partial.astype(jnp.bfloat16)
    other = lax.ppermute(own, "tp", [(0, 1), (1, 0)])
    return own.astype(jnp.float32) + other.astype(jnp.float32)


PAIR = 2 * HD
ROWS = 256


def attention_kernel(cache_len_ref, group_len_ref, x_ref, wq_ref, wk_ref, wv_ref, kc_ref, vc_ref, out_ref):
    cached = cache_len_ref[lax.axis_index("req")]
    valid = group_len_ref[0]
    x = x_ref[...]
    q_all = jnp.dot(x, wq_ref[...], preferred_element_type=jnp.float32).astype(jnp.bfloat16)
    kn = jnp.dot(x, wk_ref[...], preferred_element_type=jnp.float32).astype(jnp.bfloat16)
    vn = jnp.dot(x, wv_ref[...], preferred_element_type=jnp.float32).astype(jnp.bfloat16)
    kc = kc_ref[...]
    vc = vc_ref[...]
    scale = 1.0 / float(HD) ** 0.5
    dims = (((1,), (1,)), ((), ()))
    for chunk in range(x.shape[0] // ROWS):
        row0 = chunk * ROWS
        q = q_all[row0 : row0 + ROWS]
        reach = row0 + ROWS
        kn_seen = kn[:reach]
        vn_seen = vn[:reach]
        lanes = lax.broadcasted_iota(jnp.int32, q.shape, 1)
        cache_cols = lax.broadcasted_iota(jnp.int32, (ROWS, kc.shape[0]), 1)
        cache_ok = cache_cols < cached
        new_cols = lax.broadcasted_iota(jnp.int32, (ROWS, reach), 1)
        new_rows = lax.broadcasted_iota(jnp.int32, (ROWS, reach), 0) + row0
        new_ok = (new_cols <= new_rows) & (new_cols < valid)
        result = jnp.zeros(q.shape, jnp.float32)
        for head in range(2):
            mine = (lanes // HD) == head
            qh = jnp.where(mine, q, jnp.zeros_like(q))
            s_c = lax.dot_general(qh, kc, dims, preferred_element_type=jnp.float32) * scale
            s_n = lax.dot_general(qh, kn_seen, dims, preferred_element_type=jnp.float32) * scale
            s_c = jnp.where(cache_ok, s_c, -jnp.inf)
            s_n = jnp.where(new_ok, s_n, -jnp.inf)
            peak = jnp.maximum(
                jnp.max(s_c, axis=1, keepdims=True), jnp.max(s_n, axis=1, keepdims=True)
            )
            e_c = jnp.exp(s_c - peak)
            e_n = jnp.exp(s_n - peak)
            total = jnp.sum(e_c, axis=1, keepdims=True) + jnp.sum(e_n, axis=1, keepdims=True)
            mixed = jnp.dot(
                e_c.astype(jnp.bfloat16), vc, preferred_element_type=jnp.float32
            ) + jnp.dot(e_n.astype(jnp.bfloat16), vn_seen, preferred_element_type=jnp.float32)
            result = jnp.where(mine, mixed / total, result)
        out_ref[row0 : row0 + ROWS, :] = result.astype(out_ref.dtype)


def attention(cache_len, group_len, tokens, w_query, w_key, w_value, cache_k, cache_v):
    rows, model = tokens.shape
    width = w_query.shape[1]
    cache_rows = cache_k.shape[0]
    pairs = width // PAIR
    flops = 4 * rows * (cache_rows + rows) * width * 2 + 6 * rows * model * width
    return pl.pallas_call(
        attention_kernel,
        out_shape=jax.ShapeDtypeStruct((rows, width), jnp.bfloat16),
        grid_spec=pltpu.PrefetchScalarGridSpec(
            num_scalar_prefetch=2,
            grid=(pairs,),
            in_specs=[
                pl.BlockSpec((rows, model), lambda p, c, g: (0, 0)),
                pl.BlockSpec((model, PAIR), lambda p, c, g: (0, p)),
                pl.BlockSpec((model, PAIR), lambda p, c, g: (0, p)),
                pl.BlockSpec((model, PAIR), lambda p, c, g: (0, p)),
                pl.BlockSpec((cache_rows, PAIR), lambda p, c, g: (0, p)),
                pl.BlockSpec((cache_rows, PAIR), lambda p, c, g: (0, p)),
            ],
            out_specs=pl.BlockSpec((rows, PAIR), lambda p, c, g: (0, p)),
        ),
        cost_estimate=pl.CostEstimate(
            flops=flops,
            transcendentals=rows * (cache_rows + rows) * width // HD,
            bytes_accessed=2 * (rows * model + 3 * model * width + 2 * cache_rows * width + rows * width),
        ),
    )(cache_len, group_len, tokens, w_query, w_key, w_value, cache_k, cache_v)


NORM_ROWS = 256


def residual_norm_kernel(mid_ref, own_ref, other_ref, gain_ref, bias_ref, out_ref):
    total = own_ref[...].astype(jnp.float32) + other_ref[...].astype(jnp.float32)
    rows = mid_ref[...].astype(jnp.float32) + total
    center = rows - jnp.mean(rows, axis=-1, keepdims=True)
    spread = jnp.mean(center * center, axis=-1, keepdims=True)
    out_ref[...] = (center * lax.rsqrt(spread + 1e-05) * gain_ref[...] + bias_ref[...]).astype(
        out_ref.dtype
    )


def residual_norm(middle, own, other, gain, bias):
    rows, width = middle.shape
    block = pl.BlockSpec((NORM_ROWS, width), lambda i: (i, 0))
    vector = pl.BlockSpec((1, width), lambda i: (0, 0))
    return pl.pallas_call(
        residual_norm_kernel,
        out_shape=jax.ShapeDtypeStruct((rows, width), jnp.bfloat16),
        grid=(rows // NORM_ROWS,),
        in_specs=[block, block, block, vector, vector],
        out_specs=block,
        cost_estimate=pl.CostEstimate(
            flops=10 * rows * width, transcendentals=rows, bytes_accessed=8 * rows * width
        ),
    )(middle, own, other, gain, bias)


def shards(
    tokens,
    group_len,
    cache_len,
    cache_keys,
    cache_values,
    w_query,
    w_key,
    w_value,
    w_out,
    w_up,
    w_down,
    ln_gains,
    ln_biases,
    embed,
):
    block_rows = tokens.shape[0]
    local_width = w_query.shape[1]
    my_index = lax.axis_index("req")
    my_valid = group_len[0]
    attn_mixed = attention(cache_len, group_len, tokens, w_query, w_key, w_value, cache_keys[0], cache_values[0])
    attn_sum = pair_sum(jnp.dot(attn_mixed, w_out, preferred_element_type=jnp.float32))
    middle = normalize(tokens.astype(jnp.float32) + attn_sum, ln_gains[0], ln_biases[0]).astype(
        jnp.bfloat16
    )
    active = jax.nn.gelu(
        jnp.dot(middle, w_up, preferred_element_type=jnp.float32), approximate=False
    ).astype(jnp.bfloat16)
    own = jnp.dot(active, w_down, preferred_element_type=jnp.float32).astype(jnp.bfloat16)
    other = lax.ppermute(own, "tp", [(0, 1), (1, 0)])
    layer_out = residual_norm(middle, own, other, ln_gains[1:2], ln_biases[1:2])
    last_row = lax.dynamic_slice_in_dim(layer_out, my_valid - 1, 1, 0)
    reqs = cache_len.shape[0]
    all_rows = lax.all_to_all(
        jnp.broadcast_to(last_row, (reqs, last_row.shape[1])), "req", 0, 0, tiled=True
    )
    logits = jnp.einsum("rd,vd->rv", all_rows, embed, preferred_element_type=jnp.float32)
    slice_best = jnp.max(logits, axis=1)
    spread = jnp.repeat(slice_best, 2)[:, None]
    best_logit = jnp.max(lax.all_to_all(spread, ("req", "tp"), 0, 0, tiled=True), axis=0)
    return (layer_out, best_logit, slice_best[:, None])


def solution(mesh):
    placed = (
        P("req", None),
        P("req"),
        P(),
        P("req", None, "tp"),
        P("req", None, "tp"),
        P(None, "tp"),
        P(None, "tp"),
        P(None, "tp"),
        P("tp", None),
        P(None, "tp"),
        P("tp", None),
        P(),
        P(),
        P(("req", "tp"), None),
    )
    return jax.shard_map(
        shards,
        mesh=mesh,
        in_specs=placed,
        out_specs=(P("req", None), P("req"), P(None, ("req", "tp"))),
        check_vma=False,
    )
```

```python
import jax
import jax.numpy as jnp
from jax import lax
from jax.experimental import pallas as pl
from jax.experimental.pallas import tpu as pltpu
from jax.sharding import PartitionSpec as P

HD = 64


def normalize(rows, gain, bias):
    center = rows - jnp.mean(rows, axis=-1, keepdims=True)
    spread = jnp.mean(center * center, axis=-1, keepdims=True)
    return center * lax.rsqrt(spread + 1e-05) * gain + bias


def pair_sum(partial):
    own = partial.astype(jnp.bfloat16)
    other = lax.ppermute(own, "tp", [(0, 1), (1, 0)])
    return own.astype(jnp.float32) + other.astype(jnp.float32)


PAIR = 2 * HD
ROWS = 256


def attention_kernel(cache_len_ref, group_len_ref, x_ref, wq_ref, wk_ref, wv_ref, kc_ref, vc_ref, out_ref):
    cached = cache_len_ref[lax.axis_index("req")]
    valid = group_len_ref[0]
    x = x_ref[...]
    q_all = jnp.dot(x, wq_ref[...], preferred_element_type=jnp.float32).astype(jnp.bfloat16)
    kn = jnp.dot(x, wk_ref[...], preferred_element_type=jnp.float32).astype(jnp.bfloat16)
    vn = jnp.dot(x, wv_ref[...], preferred_element_type=jnp.float32).astype(jnp.bfloat16)
    kc = kc_ref[...]
    vc = vc_ref[...]
    scale = 1.0 / float(HD) ** 0.5
    dims = (((1,), (1,)), ((), ()))
    for chunk in range(x.shape[0] // ROWS):
        row0 = chunk * ROWS
        q = q_all[row0 : row0 + ROWS]
        reach = row0 + ROWS
        kn_seen = kn[:reach]
        vn_seen = vn[:reach]
        lanes = lax.broadcasted_iota(jnp.int32, q.shape, 1)
        cache_cols = lax.broadcasted_iota(jnp.int32, (ROWS, kc.shape[0]), 1)
        cache_ok = cache_cols < cached
        new_cols = lax.broadcasted_iota(jnp.int32, (ROWS, reach), 1)
        new_rows = lax.broadcasted_iota(jnp.int32, (ROWS, reach), 0) + row0
        new_ok = (new_cols <= new_rows) & (new_cols < valid)
        result = jnp.zeros(q.shape, jnp.float32)
        for head in range(2):
            mine = (lanes // HD) == head
            qh = jnp.where(mine, q, jnp.zeros_like(q))
            s_c = lax.dot_general(qh, kc, dims, preferred_element_type=jnp.float32) * scale
            s_n = lax.dot_general(qh, kn_seen, dims, preferred_element_type=jnp.float32) * scale
            s_c = jnp.where(cache_ok, s_c, -jnp.inf)
            s_n = jnp.where(new_ok, s_n, -jnp.inf)
            peak = jnp.maximum(
                jnp.max(s_c, axis=1, keepdims=True), jnp.max(s_n, axis=1, keepdims=True)
            )
            e_c = jnp.exp(s_c - peak)
            e_n = jnp.exp(s_n - peak)
            total = jnp.sum(e_c, axis=1, keepdims=True) + jnp.sum(e_n, axis=1, keepdims=True)
            mixed = jnp.dot(
                e_c.astype(jnp.bfloat16), vc, preferred_element_type=jnp.float32
            ) + jnp.dot(e_n.astype(jnp.bfloat16), vn_seen, preferred_element_type=jnp.float32)
            result = jnp.where(mine, mixed / total, result)
        out_ref[row0 : row0 + ROWS, :] = result.astype(out_ref.dtype)


def attention(cache_len, group_len, tokens, w_query, w_key, w_value, cache_k, cache_v):
    rows, model = tokens.shape
    width = w_query.shape[1]
    cache_rows = cache_k.shape[0]
    pairs = width // PAIR
    flops = 4 * rows * (cache_rows + rows) * width * 2 + 6 * rows * model * width
    return pl.pallas_call(
        attention_kernel,
        out_shape=jax.ShapeDtypeStruct((rows, width), jnp.bfloat16),
        grid_spec=pltpu.PrefetchScalarGridSpec(
            num_scalar_prefetch=2,
            grid=(pairs,),
            in_specs=[
                pl.BlockSpec((rows, model), lambda p, c, g: (0, 0)),
                pl.BlockSpec((model, PAIR), lambda p, c, g: (0, p)),
                pl.BlockSpec((model, PAIR), lambda p, c, g: (0, p)),
                pl.BlockSpec((model, PAIR), lambda p, c, g: (0, p)),
                pl.BlockSpec((cache_rows, PAIR), lambda p, c, g: (0, p)),
                pl.BlockSpec((cache_rows, PAIR), lambda p, c, g: (0, p)),
            ],
            out_specs=pl.BlockSpec((rows, PAIR), lambda p, c, g: (0, p)),
        ),
        cost_estimate=pl.CostEstimate(
            flops=flops,
            transcendentals=rows * (cache_rows + rows) * width // HD,
            bytes_accessed=2 * (rows * model + 3 * model * width + 2 * cache_rows * width + rows * width),
        ),
    )(cache_len, group_len, tokens, w_query, w_key, w_value, cache_k, cache_v)


NORM_ROWS = 256


def residual_norm_kernel(mid_ref, own_ref, other_ref, gain_ref, bias_ref, out_ref):
    total = own_ref[...].astype(jnp.float32) + other_ref[...].astype(jnp.float32)
    rows = mid_ref[...].astype(jnp.float32) + total
    center = rows - jnp.mean(rows, axis=-1, keepdims=True)
    spread = jnp.mean(center * center, axis=-1, keepdims=True)
    out_ref[...] = (center * lax.rsqrt(spread + 1e-05) * gain_ref[...] + bias_ref[...]).astype(
        out_ref.dtype
    )


def residual_norm(middle, own, other, gain, bias):
    rows, width = middle.shape
    block = pl.BlockSpec((NORM_ROWS, width), lambda i: (i, 0))
    vector = pl.BlockSpec((1, width), lambda i: (0, 0))
    return pl.pallas_call(
        residual_norm_kernel,
        out_shape=jax.ShapeDtypeStruct((rows, width), jnp.bfloat16),
        grid=(rows // NORM_ROWS,),
        in_specs=[block, block, block, vector, vector],
        out_specs=block,
        cost_estimate=pl.CostEstimate(
            flops=10 * rows * width, transcendentals=rows, bytes_accessed=8 * rows * width
        ),
    )(middle, own, other, gain, bias)


def shards(
    tokens,
    group_len,
    cache_len,
    cache_keys,
    cache_values,
    w_query,
    w_key,
    w_value,
    w_out,
    w_up,
    w_down,
    ln_gains,
    ln_biases,
    embed,
):
    block_rows = tokens.shape[0]
    local_width = w_query.shape[1]
    my_index = lax.axis_index("req")
    my_valid = group_len[0]
    attn_mixed = attention(cache_len, group_len, tokens, w_query, w_key, w_value, cache_keys[0], cache_values[0])
    attn_own = jnp.dot(attn_mixed, w_out, preferred_element_type=jnp.float32).astype(jnp.bfloat16)
    attn_other = lax.ppermute(attn_own, "tp", [(0, 1), (1, 0)])
    middle = residual_norm(tokens, attn_own, attn_other, ln_gains[0:1], ln_biases[0:1])
    active = jax.nn.gelu(
        jnp.dot(middle, w_up, preferred_element_type=jnp.float32), approximate=False
    ).astype(jnp.bfloat16)
    own = jnp.dot(active, w_down, preferred_element_type=jnp.float32).astype(jnp.bfloat16)
    other = lax.ppermute(own, "tp", [(0, 1), (1, 0)])
    layer_out = residual_norm(middle, own, other, ln_gains[1:2], ln_biases[1:2])
    last_row = lax.dynamic_slice_in_dim(layer_out, my_valid - 1, 1, 0)
    reqs = cache_len.shape[0]
    all_rows = lax.all_to_all(
        jnp.broadcast_to(last_row, (reqs, last_row.shape[1])), "req", 0, 0, tiled=True
    )
    logits = jnp.einsum("rd,vd->rv", all_rows, embed, preferred_element_type=jnp.float32)
    slice_best = jnp.max(logits, axis=1)
    spread = jnp.repeat(slice_best, 2)[:, None]
    best_logit = jnp.max(lax.all_to_all(spread, ("req", "tp"), 0, 0, tiled=True), axis=0)
    return (layer_out, best_logit, slice_best[:, None])


def solution(mesh):
    placed = (
        P("req", None),
        P("req"),
        P(),
        P("req", None, "tp"),
        P("req", None, "tp"),
        P(None, "tp"),
        P(None, "tp"),
        P(None, "tp"),
        P("tp", None),
        P(None, "tp"),
        P("tp", None),
        P(),
        P(),
        P(("req", "tp"), None),
    )
    return jax.shard_map(
        shards,
        mesh=mesh,
        in_specs=placed,
        out_specs=(P("req", None), P("req"), P(None, ("req", "tp"))),
        check_vma=False,
    )
```

```python
import jax
import jax.numpy as jnp
from jax import lax
from jax.experimental import pallas as pl
from jax.experimental.pallas import tpu as pltpu
from jax.sharding import PartitionSpec as P

HD = 64


def normalize(rows, gain, bias):
    center = rows - jnp.mean(rows, axis=-1, keepdims=True)
    spread = jnp.mean(center * center, axis=-1, keepdims=True)
    return center * lax.rsqrt(spread + 1e-05) * gain + bias


def pair_sum(partial):
    own = partial.astype(jnp.bfloat16)
    other = lax.ppermute(own, "tp", [(0, 1), (1, 0)])
    return own.astype(jnp.float32) + other.astype(jnp.float32)


PAIR = 2 * HD
ROWS = 256


def attention_kernel(
    cache_len_ref, group_len_ref, x_ref, wq_ref, wk_ref, wv_ref, kc_ref, vc_ref, wo_ref, out_ref, acc_ref
):
    cached = cache_len_ref[lax.axis_index("req")]
    valid = group_len_ref[0]
    x = x_ref[...]
    q_all = jnp.dot(x, wq_ref[...], preferred_element_type=jnp.float32).astype(jnp.bfloat16)
    kn = jnp.dot(x, wk_ref[...], preferred_element_type=jnp.float32).astype(jnp.bfloat16)
    vn = jnp.dot(x, wv_ref[...], preferred_element_type=jnp.float32).astype(jnp.bfloat16)
    kc = kc_ref[...]
    vc = vc_ref[...]
    wo = wo_ref[...]
    pair = pl.program_id(0)

    @pl.when(pair == 0)
    def _():
        acc_ref[...] = jnp.zeros_like(acc_ref)

    scale = 1.0 / float(HD) ** 0.5
    dims = (((1,), (1,)), ((), ()))
    for chunk in range(x.shape[0] // ROWS):
        row0 = chunk * ROWS
        q = q_all[row0 : row0 + ROWS]
        reach = row0 + ROWS
        kn_seen = kn[:reach]
        vn_seen = vn[:reach]
        lanes = lax.broadcasted_iota(jnp.int32, q.shape, 1)
        cache_cols = lax.broadcasted_iota(jnp.int32, (ROWS, kc.shape[0]), 1)
        cache_ok = cache_cols < cached
        new_cols = lax.broadcasted_iota(jnp.int32, (ROWS, reach), 1)
        new_rows = lax.broadcasted_iota(jnp.int32, (ROWS, reach), 0) + row0
        new_ok = (new_cols <= new_rows) & (new_cols < valid)
        result = jnp.zeros(q.shape, jnp.float32)
        for head in range(2):
            mine = (lanes // HD) == head
            qh = jnp.where(mine, q, jnp.zeros_like(q))
            s_c = lax.dot_general(qh, kc, dims, preferred_element_type=jnp.float32) * scale
            s_n = lax.dot_general(qh, kn_seen, dims, preferred_element_type=jnp.float32) * scale
            s_c = jnp.where(cache_ok, s_c, -jnp.inf)
            s_n = jnp.where(new_ok, s_n, -jnp.inf)
            peak = jnp.maximum(
                jnp.max(s_c, axis=1, keepdims=True), jnp.max(s_n, axis=1, keepdims=True)
            )
            e_c = jnp.exp(s_c - peak)
            e_n = jnp.exp(s_n - peak)
            total = jnp.sum(e_c, axis=1, keepdims=True) + jnp.sum(e_n, axis=1, keepdims=True)
            mixed = jnp.dot(
                e_c.astype(jnp.bfloat16), vc, preferred_element_type=jnp.float32
            ) + jnp.dot(e_n.astype(jnp.bfloat16), vn_seen, preferred_element_type=jnp.float32)
            result = jnp.where(mine, mixed / total, result)
        acc_ref[row0 : row0 + ROWS, :] += jnp.dot(
            result.astype(jnp.bfloat16), wo, preferred_element_type=jnp.float32
        )

    @pl.when(pair == pl.num_programs(0) - 1)
    def _():
        out_ref[...] = acc_ref[...].astype(out_ref.dtype)


def attention(cache_len, group_len, tokens, w_query, w_key, w_value, cache_k, cache_v, w_out):
    rows, model = tokens.shape
    width = w_query.shape[1]
    cache_rows = cache_k.shape[0]
    pairs = width // PAIR
    flops = 4 * rows * (cache_rows + rows) * width * 2 + 6 * rows * model * width
    return pl.pallas_call(
        attention_kernel,
        out_shape=jax.ShapeDtypeStruct((rows, model), jnp.bfloat16),
        grid_spec=pltpu.PrefetchScalarGridSpec(
            num_scalar_prefetch=2,
            grid=(pairs,),
            in_specs=[
                pl.BlockSpec((rows, model), lambda p, c, g: (0, 0)),
                pl.BlockSpec((model, PAIR), lambda p, c, g: (0, p)),
                pl.BlockSpec((model, PAIR), lambda p, c, g: (0, p)),
                pl.BlockSpec((model, PAIR), lambda p, c, g: (0, p)),
                pl.BlockSpec((cache_rows, PAIR), lambda p, c, g: (0, p)),
                pl.BlockSpec((cache_rows, PAIR), lambda p, c, g: (0, p)),
                pl.BlockSpec((PAIR, model), lambda p, c, g: (p, 0)),
            ],
            out_specs=pl.BlockSpec((rows, model), lambda p, c, g: (0, 0)),
            scratch_shapes=[pltpu.VMEM((rows, model), jnp.float32)],
        ),
        cost_estimate=pl.CostEstimate(
            flops=flops,
            transcendentals=rows * (cache_rows + rows) * width // HD,
            bytes_accessed=2 * (rows * model + 3 * model * width + 2 * cache_rows * width + rows * width),
        ),
    )(cache_len, group_len, tokens, w_query, w_key, w_value, cache_k, cache_v, w_out)


NORM_ROWS = 256


def residual_norm_kernel(mid_ref, own_ref, other_ref, gain_ref, bias_ref, out_ref):
    total = own_ref[...].astype(jnp.float32) + other_ref[...].astype(jnp.float32)
    rows = mid_ref[...].astype(jnp.float32) + total
    center = rows - jnp.mean(rows, axis=-1, keepdims=True)
    spread = jnp.mean(center * center, axis=-1, keepdims=True)
    out_ref[...] = (center * lax.rsqrt(spread + 1e-05) * gain_ref[...] + bias_ref[...]).astype(
        out_ref.dtype
    )


def residual_norm(middle, own, other, gain, bias):
    rows, width = middle.shape
    block = pl.BlockSpec((NORM_ROWS, width), lambda i: (i, 0))
    vector = pl.BlockSpec((1, width), lambda i: (0, 0))
    return pl.pallas_call(
        residual_norm_kernel,
        out_shape=jax.ShapeDtypeStruct((rows, width), jnp.bfloat16),
        grid=(rows // NORM_ROWS,),
        in_specs=[block, block, block, vector, vector],
        out_specs=block,
        cost_estimate=pl.CostEstimate(
            flops=10 * rows * width, transcendentals=rows, bytes_accessed=8 * rows * width
        ),
    )(middle, own, other, gain, bias)


def shards(
    tokens,
    group_len,
    cache_len,
    cache_keys,
    cache_values,
    w_query,
    w_key,
    w_value,
    w_out,
    w_up,
    w_down,
    ln_gains,
    ln_biases,
    embed,
):
    block_rows = tokens.shape[0]
    local_width = w_query.shape[1]
    my_index = lax.axis_index("req")
    my_valid = group_len[0]
    attn_own = attention(
        cache_len, group_len, tokens, w_query, w_key, w_value, cache_keys[0], cache_values[0], w_out
    )
    attn_sum = pair_sum(attn_own)
    middle = normalize(tokens.astype(jnp.float32) + attn_sum, ln_gains[0], ln_biases[0]).astype(
        jnp.bfloat16
    )
    active = jax.nn.gelu(
        jnp.dot(middle, w_up, preferred_element_type=jnp.float32), approximate=False
    ).astype(jnp.bfloat16)
    own = jnp.dot(active, w_down, preferred_element_type=jnp.float32).astype(jnp.bfloat16)
    other = lax.ppermute(own, "tp", [(0, 1), (1, 0)])
    layer_out = residual_norm(middle, own, other, ln_gains[1:2], ln_biases[1:2])
    last_row = lax.dynamic_slice_in_dim(layer_out, my_valid - 1, 1, 0)
    reqs = cache_len.shape[0]
    all_rows = lax.all_to_all(
        jnp.broadcast_to(last_row, (reqs, last_row.shape[1])), "req", 0, 0, tiled=True
    )
    logits = jnp.einsum("rd,vd->rv", all_rows, embed, preferred_element_type=jnp.float32)
    slice_best = jnp.max(logits, axis=1)
    spread = jnp.repeat(slice_best, 2)[:, None]
    best_logit = jnp.max(lax.all_to_all(spread, ("req", "tp"), 0, 0, tiled=True), axis=0)
    return (layer_out, best_logit, slice_best[:, None])


def solution(mesh):
    placed = (
        P("req", None),
        P("req"),
        P(),
        P("req", None, "tp"),
        P("req", None, "tp"),
        P(None, "tp"),
        P(None, "tp"),
        P(None, "tp"),
        P("tp", None),
        P(None, "tp"),
        P("tp", None),
        P(),
        P(),
        P(("req", "tp"), None),
    )
    return jax.shard_map(
        shards,
        mesh=mesh,
        in_specs=placed,
        out_specs=(P("req", None), P("req"), P(None, ("req", "tp"))),
        check_vma=False,
    )
```

```python
import jax
import jax.numpy as jnp
from jax import lax
from jax.experimental import pallas as pl
from jax.experimental.pallas import tpu as pltpu
from jax.sharding import PartitionSpec as P

HD = 64


def normalize(rows, gain, bias):
    center = rows - jnp.mean(rows, axis=-1, keepdims=True)
    spread = jnp.mean(center * center, axis=-1, keepdims=True)
    return center * lax.rsqrt(spread + 1e-05) * gain + bias


def pair_sum(partial):
    own = partial.astype(jnp.bfloat16)
    other = lax.ppermute(own, "tp", [(0, 1), (1, 0)])
    return own.astype(jnp.float32) + other.astype(jnp.float32)


PAIR = 2 * HD
ROWS = 256


def attention_kernel(cache_len_ref, group_len_ref, x_ref, wq_ref, wk_ref, wv_ref, kc_ref, vc_ref, out_ref):
    cached = cache_len_ref[lax.axis_index("req")]
    valid = group_len_ref[0]
    x = x_ref[...]
    q_all = jnp.dot(x, wq_ref[...], preferred_element_type=jnp.float32).astype(jnp.bfloat16)
    kn = jnp.dot(x, wk_ref[...], preferred_element_type=jnp.float32).astype(jnp.bfloat16)
    vn = jnp.dot(x, wv_ref[...], preferred_element_type=jnp.float32).astype(jnp.bfloat16)
    kc = kc_ref[...]
    vc = vc_ref[...]
    scale = 1.0 / float(HD) ** 0.5
    dims = (((1,), (1,)), ((), ()))
    for chunk in range(x.shape[0] // ROWS):
        row0 = chunk * ROWS
        q = q_all[row0 : row0 + ROWS]
        reach = row0 + ROWS
        kn_seen = kn[:reach]
        vn_seen = vn[:reach]
        lanes = lax.broadcasted_iota(jnp.int32, q.shape, 1)
        cache_cols = lax.broadcasted_iota(jnp.int32, (ROWS, kc.shape[0]), 1)
        cache_ok = cache_cols < cached
        new_cols = lax.broadcasted_iota(jnp.int32, (ROWS, reach), 1)
        new_rows = lax.broadcasted_iota(jnp.int32, (ROWS, reach), 0) + row0
        new_ok = (new_cols <= new_rows) & (new_cols < valid)
        result = jnp.zeros(q.shape, jnp.float32)
        for head in range(2):
            mine = (lanes // HD) == head
            qh = jnp.where(mine, q, jnp.zeros_like(q))
            s_c = lax.dot_general(qh, kc, dims, preferred_element_type=jnp.float32) * scale
            s_n = lax.dot_general(qh, kn_seen, dims, preferred_element_type=jnp.float32) * scale
            s_c = jnp.where(cache_ok, s_c, -jnp.inf)
            s_n = jnp.where(new_ok, s_n, -jnp.inf)
            peak = jnp.maximum(
                jnp.max(s_c, axis=1, keepdims=True), jnp.max(s_n, axis=1, keepdims=True)
            )
            e_c = jnp.exp(s_c - peak)
            e_n = jnp.exp(s_n - peak)
            total = jnp.sum(e_c, axis=1, keepdims=True) + jnp.sum(e_n, axis=1, keepdims=True)
            mixed = jnp.dot(
                e_c.astype(jnp.bfloat16), vc, preferred_element_type=jnp.float32
            ) + jnp.dot(e_n.astype(jnp.bfloat16), vn_seen, preferred_element_type=jnp.float32)
            result = jnp.where(mine, mixed / total, result)
        out_ref[row0 : row0 + ROWS, :] = result.astype(out_ref.dtype)


def attention(cache_len, group_len, tokens, w_query, w_key, w_value, cache_k, cache_v):
    rows, model = tokens.shape
    width = w_query.shape[1]
    cache_rows = cache_k.shape[0]
    pairs = width // PAIR
    flops = 4 * rows * (cache_rows + rows) * width * 2 + 6 * rows * model * width
    return pl.pallas_call(
        attention_kernel,
        out_shape=jax.ShapeDtypeStruct((rows, width), jnp.bfloat16),
        grid_spec=pltpu.PrefetchScalarGridSpec(
            num_scalar_prefetch=2,
            grid=(pairs,),
            in_specs=[
                pl.BlockSpec((rows, model), lambda p, c, g: (0, 0)),
                pl.BlockSpec((model, PAIR), lambda p, c, g: (0, p)),
                pl.BlockSpec((model, PAIR), lambda p, c, g: (0, p)),
                pl.BlockSpec((model, PAIR), lambda p, c, g: (0, p)),
                pl.BlockSpec((cache_rows, PAIR), lambda p, c, g: (0, p)),
                pl.BlockSpec((cache_rows, PAIR), lambda p, c, g: (0, p)),
            ],
            out_specs=pl.BlockSpec((rows, PAIR), lambda p, c, g: (0, p)),
        ),
        cost_estimate=pl.CostEstimate(
            flops=flops,
            transcendentals=rows * (cache_rows + rows) * width // HD,
            bytes_accessed=2 * (rows * model + 3 * model * width + 2 * cache_rows * width + rows * width),
        ),
    )(cache_len, group_len, tokens, w_query, w_key, w_value, cache_k, cache_v)


NORM_ROWS = 128


def residual_norm_kernel(mid_ref, own_ref, other_ref, gain_ref, bias_ref, out_ref):
    total = own_ref[...].astype(jnp.float32) + other_ref[...].astype(jnp.float32)
    rows = mid_ref[...].astype(jnp.float32) + total
    center = rows - jnp.mean(rows, axis=-1, keepdims=True)
    spread = jnp.mean(center * center, axis=-1, keepdims=True)
    out_ref[...] = (center * lax.rsqrt(spread + 1e-05) * gain_ref[...] + bias_ref[...]).astype(
        out_ref.dtype
    )


def residual_norm(middle, own, other, gain, bias):
    rows, width = middle.shape
    block = pl.BlockSpec((NORM_ROWS, width), lambda i: (i, 0))
    vector = pl.BlockSpec((1, width), lambda i: (0, 0))
    return pl.pallas_call(
        residual_norm_kernel,
        out_shape=jax.ShapeDtypeStruct((rows, width), jnp.bfloat16),
        grid=(rows // NORM_ROWS,),
        in_specs=[block, block, block, vector, vector],
        out_specs=block,
        cost_estimate=pl.CostEstimate(
            flops=10 * rows * width, transcendentals=rows, bytes_accessed=8 * rows * width
        ),
    )(middle, own, other, gain, bias)


def shards(
    tokens,
    group_len,
    cache_len,
    cache_keys,
    cache_values,
    w_query,
    w_key,
    w_value,
    w_out,
    w_up,
    w_down,
    ln_gains,
    ln_biases,
    embed,
):
    block_rows = tokens.shape[0]
    local_width = w_query.shape[1]
    my_index = lax.axis_index("req")
    my_valid = group_len[0]
    attn_mixed = attention(cache_len, group_len, tokens, w_query, w_key, w_value, cache_keys[0], cache_values[0])
    attn_sum = pair_sum(jnp.dot(attn_mixed, w_out, preferred_element_type=jnp.float32))
    middle = normalize(tokens.astype(jnp.float32) + attn_sum, ln_gains[0], ln_biases[0]).astype(
        jnp.bfloat16
    )
    active = jax.nn.gelu(
        jnp.dot(middle, w_up, preferred_element_type=jnp.float32), approximate=False
    ).astype(jnp.bfloat16)
    own = jnp.dot(active, w_down, preferred_element_type=jnp.float32).astype(jnp.bfloat16)
    other = lax.ppermute(own, "tp", [(0, 1), (1, 0)])
    layer_out = residual_norm(middle, own, other, ln_gains[1:2], ln_biases[1:2])
    last_row = lax.dynamic_slice_in_dim(layer_out, my_valid - 1, 1, 0)
    reqs = cache_len.shape[0]
    all_rows = lax.all_to_all(
        jnp.broadcast_to(last_row, (reqs, last_row.shape[1])), "req", 0, 0, tiled=True
    )
    logits = jnp.einsum("rd,vd->rv", all_rows, embed, preferred_element_type=jnp.float32)
    slice_best = jnp.max(logits, axis=1)
    spread = jnp.repeat(slice_best, 2)[:, None]
    best_logit = jnp.max(lax.all_to_all(spread, ("req", "tp"), 0, 0, tiled=True), axis=0)
    return (layer_out, best_logit, slice_best[:, None])


def solution(mesh):
    placed = (
        P("req", None),
        P("req"),
        P(),
        P("req", None, "tp"),
        P("req", None, "tp"),
        P(None, "tp"),
        P(None, "tp"),
        P(None, "tp"),
        P("tp", None),
        P(None, "tp"),
        P("tp", None),
        P(),
        P(),
        P(("req", "tp"), None),
    )
    return jax.shard_map(
        shards,
        mesh=mesh,
        in_specs=placed,
        out_specs=(P("req", None), P("req"), P(None, ("req", "tp"))),
        check_vma=False,
    )
```

```python
import jax
import jax.numpy as jnp
from jax import lax
from jax.experimental import pallas as pl
from jax.experimental.pallas import tpu as pltpu
from jax.sharding import PartitionSpec as P

HD = 64


def normalize(rows, gain, bias):
    center = rows - jnp.mean(rows, axis=-1, keepdims=True)
    spread = jnp.mean(center * center, axis=-1, keepdims=True)
    return center * lax.rsqrt(spread + 1e-05) * gain + bias


def pair_sum(partial):
    own = partial.astype(jnp.bfloat16)
    other = lax.ppermute(own, "tp", [(0, 1), (1, 0)])
    return own.astype(jnp.float32) + other.astype(jnp.float32)


PAIR = 2 * HD
ROWS = 256


def attention_kernel(cache_len_ref, group_len_ref, x_ref, wq_ref, wk_ref, wv_ref, kc_ref, vc_ref, out_ref):
    cached = cache_len_ref[lax.axis_index("req")]
    valid = group_len_ref[0]
    x = x_ref[...]
    q_all = jnp.dot(x, wq_ref[...], preferred_element_type=jnp.float32).astype(jnp.bfloat16)
    kn = jnp.dot(x, wk_ref[...], preferred_element_type=jnp.float32).astype(jnp.bfloat16)
    vn = jnp.dot(x, wv_ref[...], preferred_element_type=jnp.float32).astype(jnp.bfloat16)
    kc = kc_ref[...]
    vc = vc_ref[...]
    scale = 1.0 / float(HD) ** 0.5
    dims = (((1,), (1,)), ((), ()))
    for chunk in range(x.shape[0] // ROWS):
        row0 = chunk * ROWS
        q = q_all[row0 : row0 + ROWS]
        reach = row0 + ROWS
        kn_seen = kn[:reach]
        vn_seen = vn[:reach]
        lanes = lax.broadcasted_iota(jnp.int32, q.shape, 1)
        cache_cols = lax.broadcasted_iota(jnp.int32, (ROWS, kc.shape[0]), 1)
        cache_ok = cache_cols < cached
        new_cols = lax.broadcasted_iota(jnp.int32, (ROWS, reach), 1)
        new_rows = lax.broadcasted_iota(jnp.int32, (ROWS, reach), 0) + row0
        new_ok = (new_cols <= new_rows) & (new_cols < valid)
        result = jnp.zeros(q.shape, jnp.float32)
        for head in range(2):
            mine = (lanes // HD) == head
            qh = jnp.where(mine, q, jnp.zeros_like(q))
            s_c = lax.dot_general(qh, kc, dims, preferred_element_type=jnp.float32) * scale
            s_n = lax.dot_general(qh, kn_seen, dims, preferred_element_type=jnp.float32) * scale
            s_c = jnp.where(cache_ok, s_c, -jnp.inf)
            s_n = jnp.where(new_ok, s_n, -jnp.inf)
            peak = jnp.maximum(
                jnp.max(s_c, axis=1, keepdims=True), jnp.max(s_n, axis=1, keepdims=True)
            )
            e_c = jnp.exp(s_c - peak)
            e_n = jnp.exp(s_n - peak)
            total = jnp.sum(e_c, axis=1, keepdims=True) + jnp.sum(e_n, axis=1, keepdims=True)
            mixed = jnp.dot(
                e_c.astype(jnp.bfloat16), vc, preferred_element_type=jnp.float32
            ) + jnp.dot(e_n.astype(jnp.bfloat16), vn_seen, preferred_element_type=jnp.float32)
            result = jnp.where(mine, mixed / total, result)
        out_ref[row0 : row0 + ROWS, :] = result.astype(out_ref.dtype)


def attention(cache_len, group_len, tokens, w_query, w_key, w_value, cache_k, cache_v):
    rows, model = tokens.shape
    width = w_query.shape[1]
    cache_rows = cache_k.shape[0]
    pairs = width // PAIR
    flops = 4 * rows * (cache_rows + rows) * width * 2 + 6 * rows * model * width
    return pl.pallas_call(
        attention_kernel,
        out_shape=jax.ShapeDtypeStruct((rows, width), jnp.bfloat16),
        grid_spec=pltpu.PrefetchScalarGridSpec(
            num_scalar_prefetch=2,
            grid=(pairs,),
            in_specs=[
                pl.BlockSpec((rows, model), lambda p, c, g: (0, 0)),
                pl.BlockSpec((model, PAIR), lambda p, c, g: (0, p)),
                pl.BlockSpec((model, PAIR), lambda p, c, g: (0, p)),
                pl.BlockSpec((model, PAIR), lambda p, c, g: (0, p)),
                pl.BlockSpec((cache_rows, PAIR), lambda p, c, g: (0, p)),
                pl.BlockSpec((cache_rows, PAIR), lambda p, c, g: (0, p)),
            ],
            out_specs=pl.BlockSpec((rows, PAIR), lambda p, c, g: (0, p)),
        ),
        cost_estimate=pl.CostEstimate(
            flops=flops,
            transcendentals=rows * (cache_rows + rows) * width // HD,
            bytes_accessed=2 * (rows * model + 3 * model * width + 2 * cache_rows * width + rows * width),
        ),
    )(cache_len, group_len, tokens, w_query, w_key, w_value, cache_k, cache_v)


NORM_ROWS = 256


def residual_norm_kernel(group_len_ref, mid_ref, own_ref, other_ref, gain_ref, bias_ref, out_ref, copies_ref):
    total = own_ref[...].astype(jnp.float32) + other_ref[...].astype(jnp.float32)
    rows = mid_ref[...].astype(jnp.float32) + total
    center = rows - jnp.mean(rows, axis=-1, keepdims=True)
    spread = jnp.mean(center * center, axis=-1, keepdims=True)
    out_ref[...] = (center * lax.rsqrt(spread + 1e-05) * gain_ref[...] + bias_ref[...]).astype(
        out_ref.dtype
    )
    last = group_len_ref[0] - 1

    @pl.when(last // NORM_ROWS == pl.program_id(0))
    def _():
        within = last % NORM_ROWS
        start = pl.multiple_of((within // 16) * 16, 16)
        window = out_ref[pl.ds(start, 16), :].astype(jnp.float32)
        pick = lax.broadcasted_iota(jnp.int32, window.shape, 0) == within - start
        row = jnp.sum(jnp.where(pick, window, 0.0), axis=0, keepdims=True)
        copies_ref[...] = jnp.broadcast_to(row, copies_ref.shape).astype(copies_ref.dtype)


def residual_norm(group_len, middle, own, other, gain, bias, reqs):
    rows, width = middle.shape
    block = pl.BlockSpec((NORM_ROWS, width), lambda i, g: (i, 0))
    vector = pl.BlockSpec((1, width), lambda i, g: (0, 0))
    return pl.pallas_call(
        residual_norm_kernel,
        out_shape=(
            jax.ShapeDtypeStruct((rows, width), jnp.bfloat16),
            jax.ShapeDtypeStruct((reqs, width), jnp.bfloat16),
        ),
        grid_spec=pltpu.PrefetchScalarGridSpec(
            num_scalar_prefetch=1,
            grid=(rows // NORM_ROWS,),
            in_specs=[block, block, block, vector, vector],
            out_specs=(block, pl.BlockSpec((reqs, width), lambda i, g: (0, 0))),
        ),
        cost_estimate=pl.CostEstimate(
            flops=10 * rows * width, transcendentals=rows, bytes_accessed=8 * rows * width
        ),
    )(group_len, middle, own, other, gain, bias)


def shards(
    tokens,
    group_len,
    cache_len,
    cache_keys,
    cache_values,
    w_query,
    w_key,
    w_value,
    w_out,
    w_up,
    w_down,
    ln_gains,
    ln_biases,
    embed,
):
    block_rows = tokens.shape[0]
    local_width = w_query.shape[1]
    my_index = lax.axis_index("req")
    my_valid = group_len[0]
    attn_mixed = attention(cache_len, group_len, tokens, w_query, w_key, w_value, cache_keys[0], cache_values[0])
    attn_sum = pair_sum(jnp.dot(attn_mixed, w_out, preferred_element_type=jnp.float32))
    middle = normalize(tokens.astype(jnp.float32) + attn_sum, ln_gains[0], ln_biases[0]).astype(
        jnp.bfloat16
    )
    active = jax.nn.gelu(
        jnp.dot(middle, w_up, preferred_element_type=jnp.float32), approximate=False
    ).astype(jnp.bfloat16)
    own = jnp.dot(active, w_down, preferred_element_type=jnp.float32).astype(jnp.bfloat16)
    other = lax.ppermute(own, "tp", [(0, 1), (1, 0)])
    layer_out, copies = residual_norm(
        group_len, middle, own, other, ln_gains[1:2], ln_biases[1:2], cache_len.shape[0]
    )
    reqs = cache_len.shape[0]
    all_rows = lax.all_to_all(copies, "req", 0, 0, tiled=True)
    logits = jnp.einsum("rd,vd->rv", all_rows, embed, preferred_element_type=jnp.float32)
    slice_best = jnp.max(logits, axis=1)
    spread = jnp.repeat(slice_best, 2)[:, None]
    best_logit = jnp.max(lax.all_to_all(spread, ("req", "tp"), 0, 0, tiled=True), axis=0)
    return (layer_out, best_logit, slice_best[:, None])


def solution(mesh):
    placed = (
        P("req", None),
        P("req"),
        P(),
        P("req", None, "tp"),
        P("req", None, "tp"),
        P(None, "tp"),
        P(None, "tp"),
        P(None, "tp"),
        P("tp", None),
        P(None, "tp"),
        P("tp", None),
        P(),
        P(),
        P(("req", "tp"), None),
    )
    return jax.shard_map(
        shards,
        mesh=mesh,
        in_specs=placed,
        out_specs=(P("req", None), P("req"), P(None, ("req", "tp"))),
        check_vma=False,
    )
```

```python
import jax
import jax.numpy as jnp
from jax import lax
from jax.experimental import pallas as pl
from jax.experimental.pallas import tpu as pltpu
from jax.sharding import PartitionSpec as P

HD = 64


def normalize(rows, gain, bias):
    center = rows - jnp.mean(rows, axis=-1, keepdims=True)
    spread = jnp.mean(center * center, axis=-1, keepdims=True)
    return center * lax.rsqrt(spread + 1e-05) * gain + bias


def pair_sum(partial):
    own = partial.astype(jnp.bfloat16)
    other = lax.ppermute(own, "tp", [(0, 1), (1, 0)])
    return own.astype(jnp.float32) + other.astype(jnp.float32)


PAIR = 2 * HD
ROWS = 256


def attention_kernel(cache_len_ref, group_len_ref, x_ref, wq_ref, wk_ref, wv_ref, kc_ref, vc_ref, out_ref):
    cached = cache_len_ref[lax.axis_index("req")]
    valid = group_len_ref[0]
    x = x_ref[...]
    q_all = jnp.dot(x, wq_ref[...], preferred_element_type=jnp.float32).astype(jnp.bfloat16)
    kn = jnp.dot(x, wk_ref[...], preferred_element_type=jnp.float32).astype(jnp.bfloat16)
    vn = jnp.dot(x, wv_ref[...], preferred_element_type=jnp.float32).astype(jnp.bfloat16)
    kc = kc_ref[...]
    vc = vc_ref[...]
    scale = 1.0 / float(HD) ** 0.5
    dims = (((1,), (1,)), ((), ()))
    for chunk in range(x.shape[0] // ROWS):
        row0 = chunk * ROWS
        q = q_all[row0 : row0 + ROWS]
        reach = row0 + ROWS
        kn_seen = kn[:reach]
        vn_seen = vn[:reach]
        lanes = lax.broadcasted_iota(jnp.int32, q.shape, 1)
        cache_cols = lax.broadcasted_iota(jnp.int32, (ROWS, kc.shape[0]), 1)
        cache_ok = cache_cols < cached
        new_cols = lax.broadcasted_iota(jnp.int32, (ROWS, reach), 1)
        new_rows = lax.broadcasted_iota(jnp.int32, (ROWS, reach), 0) + row0
        new_ok = (new_cols <= new_rows) & (new_cols < valid)
        result = jnp.zeros(q.shape, jnp.float32)
        for head in range(2):
            mine = (lanes // HD) == head
            qh = jnp.where(mine, q, jnp.zeros_like(q))
            s_c = lax.dot_general(qh, kc, dims, preferred_element_type=jnp.float32) * scale
            s_n = lax.dot_general(qh, kn_seen, dims, preferred_element_type=jnp.float32) * scale
            s_c = jnp.where(cache_ok, s_c, -jnp.inf)
            s_n = jnp.where(new_ok, s_n, -jnp.inf)
            peak = jnp.maximum(
                jnp.max(s_c, axis=1, keepdims=True), jnp.max(s_n, axis=1, keepdims=True)
            )
            e_c = jnp.exp(s_c - peak)
            e_n = jnp.exp(s_n - peak)
            total = jnp.sum(e_c, axis=1, keepdims=True) + jnp.sum(e_n, axis=1, keepdims=True)
            mixed = jnp.dot(
                e_c.astype(jnp.bfloat16), vc, preferred_element_type=jnp.float32
            ) + jnp.dot(e_n.astype(jnp.bfloat16), vn_seen, preferred_element_type=jnp.float32)
            result = jnp.where(mine, mixed / total, result)
        out_ref[row0 : row0 + ROWS, :] = result.astype(out_ref.dtype)


def attention(cache_len, group_len, tokens, w_query, w_key, w_value, cache_k, cache_v):
    rows, model = tokens.shape
    width = w_query.shape[1]
    cache_rows = cache_k.shape[0]
    pairs = width // PAIR
    flops = 4 * rows * (cache_rows + rows) * width * 2 + 6 * rows * model * width
    return pl.pallas_call(
        attention_kernel,
        out_shape=jax.ShapeDtypeStruct((rows, width), jnp.bfloat16),
        grid_spec=pltpu.PrefetchScalarGridSpec(
            num_scalar_prefetch=2,
            grid=(pairs,),
            in_specs=[
                pl.BlockSpec((rows, model), lambda p, c, g: (0, 0)),
                pl.BlockSpec((model, PAIR), lambda p, c, g: (0, p)),
                pl.BlockSpec((model, PAIR), lambda p, c, g: (0, p)),
                pl.BlockSpec((model, PAIR), lambda p, c, g: (0, p)),
                pl.BlockSpec((cache_rows, PAIR), lambda p, c, g: (0, p)),
                pl.BlockSpec((cache_rows, PAIR), lambda p, c, g: (0, p)),
            ],
            out_specs=pl.BlockSpec((rows, PAIR), lambda p, c, g: (0, p)),
        ),
        cost_estimate=pl.CostEstimate(
            flops=flops,
            transcendentals=rows * (cache_rows + rows) * width // HD,
            bytes_accessed=2 * (rows * model + 3 * model * width + 2 * cache_rows * width + rows * width),
        ),
    )(cache_len, group_len, tokens, w_query, w_key, w_value, cache_k, cache_v)


NORM_ROWS = 512


def residual_norm_kernel(group_len_ref, mid_ref, own_ref, other_ref, gain_ref, bias_ref, out_ref, copies_ref):
    total = own_ref[...].astype(jnp.float32) + other_ref[...].astype(jnp.float32)
    rows = mid_ref[...].astype(jnp.float32) + total
    center = rows - jnp.mean(rows, axis=-1, keepdims=True)
    spread = jnp.mean(center * center, axis=-1, keepdims=True)
    out_ref[...] = (center * lax.rsqrt(spread + 1e-05) * gain_ref[...] + bias_ref[...]).astype(
        out_ref.dtype
    )
    last = group_len_ref[0] - 1

    @pl.when(last // NORM_ROWS == pl.program_id(0))
    def _():
        within = last % NORM_ROWS
        start = pl.multiple_of((within // 16) * 16, 16)
        window = out_ref[pl.ds(start, 16), :].astype(jnp.float32)
        pick = lax.broadcasted_iota(jnp.int32, window.shape, 0) == within - start
        row = jnp.sum(jnp.where(pick, window, 0.0), axis=0, keepdims=True)
        copies_ref[...] = jnp.broadcast_to(row, copies_ref.shape).astype(copies_ref.dtype)


def residual_norm(group_len, middle, own, other, gain, bias, reqs):
    rows, width = middle.shape
    block = pl.BlockSpec((NORM_ROWS, width), lambda i, g: (i, 0))
    vector = pl.BlockSpec((1, width), lambda i, g: (0, 0))
    return pl.pallas_call(
        residual_norm_kernel,
        out_shape=(
            jax.ShapeDtypeStruct((rows, width), jnp.bfloat16),
            jax.ShapeDtypeStruct((reqs, width), jnp.bfloat16),
        ),
        grid_spec=pltpu.PrefetchScalarGridSpec(
            num_scalar_prefetch=1,
            grid=(rows // NORM_ROWS,),
            in_specs=[block, block, block, vector, vector],
            out_specs=(block, pl.BlockSpec((reqs, width), lambda i, g: (0, 0))),
        ),
        cost_estimate=pl.CostEstimate(
            flops=10 * rows * width, transcendentals=rows, bytes_accessed=8 * rows * width
        ),
    )(group_len, middle, own, other, gain, bias)


def shards(
    tokens,
    group_len,
    cache_len,
    cache_keys,
    cache_values,
    w_query,
    w_key,
    w_value,
    w_out,
    w_up,
    w_down,
    ln_gains,
    ln_biases,
    embed,
):
    block_rows = tokens.shape[0]
    local_width = w_query.shape[1]
    my_index = lax.axis_index("req")
    my_valid = group_len[0]
    attn_mixed = attention(cache_len, group_len, tokens, w_query, w_key, w_value, cache_keys[0], cache_values[0])
    attn_sum = pair_sum(jnp.dot(attn_mixed, w_out, preferred_element_type=jnp.float32))
    middle = normalize(tokens.astype(jnp.float32) + attn_sum, ln_gains[0], ln_biases[0]).astype(
        jnp.bfloat16
    )
    active = jax.nn.gelu(
        jnp.dot(middle, w_up, preferred_element_type=jnp.float32), approximate=False
    ).astype(jnp.bfloat16)
    own = jnp.dot(active, w_down, preferred_element_type=jnp.float32).astype(jnp.bfloat16)
    other = lax.ppermute(own, "tp", [(0, 1), (1, 0)])
    layer_out, copies = residual_norm(
        group_len, middle, own, other, ln_gains[1:2], ln_biases[1:2], cache_len.shape[0]
    )
    reqs = cache_len.shape[0]
    all_rows = lax.all_to_all(copies, "req", 0, 0, tiled=True)
    logits = jnp.einsum("rd,vd->rv", all_rows, embed, preferred_element_type=jnp.float32)
    slice_best = jnp.max(logits, axis=1)
    spread = jnp.repeat(slice_best, 2)[:, None]
    best_logit = jnp.max(lax.all_to_all(spread, ("req", "tp"), 0, 0, tiled=True), axis=0)
    return (layer_out, best_logit, slice_best[:, None])


def solution(mesh):
    placed = (
        P("req", None),
        P("req"),
        P(),
        P("req", None, "tp"),
        P("req", None, "tp"),
        P(None, "tp"),
        P(None, "tp"),
        P(None, "tp"),
        P("tp", None),
        P(None, "tp"),
        P("tp", None),
        P(),
        P(),
        P(("req", "tp"), None),
    )
    return jax.shard_map(
        shards,
        mesh=mesh,
        in_specs=placed,
        out_specs=(P("req", None), P("req"), P(None, ("req", "tp"))),
        check_vma=False,
    )
```
